256 devices in a mesh: seq: 32 (over x, z), heads: 8 (over y, core).
Axes of the slice: x: 4, y: 4, z: 8, core: 2. Of those that a mesh axis runs over, the one named last changes fastest.
Arguments:
- queries: bfloat16 [8192, 4096], P('seq', 'heads'), may hold values from -8 to 8
- keys: bfloat16 [8192, 4096], P('seq', 'heads'), may hold values from -8 to 8
- values: bfloat16 [8192, 4096], P('seq', 'heads'), may hold values from -8 to 8
- w_out: bfloat16 [4096, 4096], P('heads'), may hold values from -0.09375 to 0.09375
- out_cotangent: bfloat16 [8192, 4096], P('seq', 'heads'), may hold values from -6 to 6
Outputs:
- attn: bfloat16 [8192, 4096], P('seq', 'heads')
- q_grad: bfloat16 [8192, 4096], P('seq', 'heads')
- k_grad: bfloat16 [8192, 4096], P('seq', 'heads')
- v_grad: bfloat16 [8192, 4096], P('seq', 'heads')
- w_out_grad: float32 [4096, 4096], P('seq', 'heads')
The draws below stay inside these ranges and needn't reach their ends.
All inputs are finite; a program needn't handle non-finite values.
Results may differ from the reference program's by a relative error of at most 0.008.
Values may be sent and summed in bfloat16 or wider, within the bound.
No kernel may reach another device: no remote copies, remote signals or barrier semaphores. Data moves between devices by JAX's collectives and lax.ppermute only.
A program may use at most 128 MiB of HBM per device.

```python
import math
import jax
import jax.numpy as jnp
from jax import lax

D = 4096
HEADS = 32
HEAD_DIM = 128
BLOCK = 128
TOK_DEV = 256
TOKENS = 8192


def region_field(key, offset_span):
    width = HEADS * HEAD_DIM
    regions = TOKENS // TOK_DEV
    noise = jax.random.truncated_normal(jax.random.fold_in(key, 1), -3.0, 3.0, (TOKENS, width), jnp.float32)
    offsets = jax.random.uniform(jax.random.fold_in(key, 3), (regions, 1, width), jnp.float32, -offset_span, offset_span)
    return (noise.reshape(regions, TOK_DEV, width) + offsets).reshape(TOKENS, width)


def draw_queries(key, part):
    field = region_field(jax.random.fold_in(key, 100), 1.0)
    return field.astype(jnp.bfloat16)


def draw_keys(key, part):
    field = region_field(jax.random.fold_in(key, 200), 1.0)
    return field.astype(jnp.bfloat16)


def draw_values(key, part):
    return region_field(jax.random.fold_in(key, 300), 1.5).astype(jnp.bfloat16)


def strengthened(drawn, key, source, target, shards_of, factor):
    owner, partner = [(jnp.arange(drawn.shape[axis_at]) // (drawn.shape[axis_at] // shards_of)).reshape([-1 if axis == axis_at else 1 for axis in range(drawn.ndim)]) for axis_at in (source, target)]
    chosen = jax.random.permutation(key, shards_of)[partner]
    strong = (owner == chosen) | (owner == (partner + shards_of // 2) % shards_of)
    return jnp.where(strong, factor * drawn, drawn)


def shard_levels(key, extent, split, smallest, top_value):
    loudness = 1.0
    for dim, shards_of in split:
        draws = jax.random.uniform(jax.random.fold_in(jax.random.fold_in(key, 6), dim), (shards_of,), jnp.float32, smallest / len(split), top_value / len(split))
        loudness = loudness * jnp.repeat(jnp.exp(draws), extent[dim] // shards_of).reshape((-1,) + (1,) * (len(extent) - 1 - dim))
    return loudness


def gaussian(key, dims, scale, reach, split=(), held_as=jnp.bfloat16):
    entries = scale * jax.random.normal(key, dims, jnp.float32)
    if split:
        entries = entries * shard_levels(key, dims, split, -0.22, 0.18)
    return jnp.clip(entries, -reach, reach).astype(held_as)


def bell_draw_with(key, dims, scale, most, shards, heavy, dtype=jnp.bfloat16):
    values = scale * jax.random.normal(key, dims, jnp.float32)
    if shards:
        values = values * shard_levels(key, dims, shards, -0.22, 0.18)
    return jnp.clip(strengthened(values, jax.random.fold_in(key, 3), *heavy), -most, most).astype(dtype)


def setup_inputs(seed: int = 0) -> dict:
    arg_keys = jax.random.split(jax.random.key(seed), 6)
    queries = draw_queries(jax.random.fold_in(arg_keys[5], 71), 0)
    keys = draw_keys(jax.random.fold_in(arg_keys[5], 71), 0)
    values = draw_values(jax.random.fold_in(arg_keys[5], 71), 0)
    w_out = gaussian(arg_keys[3], (HEADS * HEAD_DIM, D), (HEADS * HEAD_DIM) ** -0.5, 0.09375, ((0, 8),))
    out_cotangent = bell_draw_with(arg_keys[4], (TOKENS, D), 1.0, 6.0, ((0, 32), (1, 8)), (0, 1, 32, 2.75))
    return {"queries": queries, "keys": keys, "values": values, "w_out": w_out, "out_cotangent": out_cotangent}


highest = lax.Precision.HIGHEST

def pooled(field, level):
    length, width = field.shape
    return field.reshape(length >> level, 1 << level, width).mean(1)

def level_terms(query_units, key_units, value_units, level):
    units, width = query_units.shape
    pairs = units // (2 * BLOCK)
    scale = 1.0 / math.sqrt(HEAD_DIM)
    query_blocks = query_units.reshape(pairs, 2, BLOCK, width)
    if level == 0:
        key_blocks = key_units.reshape(pairs, 2 * BLOCK, width)
        value_blocks = value_units.reshape(pairs, 2 * BLOCK, width)
        scores = jnp.einsum('psqe,pke->psqk', query_blocks, key_blocks, precision=highest) * scale
    else:
        key_blocks = jnp.flip(key_units.reshape(pairs, 2, BLOCK, width), 1)
        value_blocks = jnp.flip(value_units.reshape(pairs, 2, BLOCK, width), 1)
        scores = jnp.einsum('psqe,pske->psqk', query_blocks, key_blocks, precision=highest) * scale
    top = lax.stop_gradient(lax.optimization_barrier(jnp.max(scores, -1)))
    weights = 2.0 ** level * jnp.exp(scores - top[..., None])
    if level == 0:
        numer = jnp.einsum('psqk,pke->psqe', weights, value_blocks, precision=highest)
    else:
        numer = jnp.einsum('psqk,pske->psqe', weights, value_blocks, precision=highest)
    return (top.reshape(units), numer.reshape(units, width), weights.sum(-1).reshape(units))

def head_attention(query, key_field, value):
    length, width = query.shape
    count = (length // BLOCK).bit_length() - 1
    stats = [level_terms(pooled(query, level), pooled(key_field, level), pooled(value, level), level) for level in range(count)]
    peak = stats[0][0]
    for level in range(1, count):
        peak = jnp.maximum(peak.reshape(length >> level, 1 << level), stats[level][0][:, None]).reshape(length)
    peak = lax.stop_gradient(peak)
    numer = jnp.zeros((length, width), jnp.float32)
    denom = jnp.zeros((length,), jnp.float32)
    for level in range(count):
        rescale = jnp.exp(stats[level][0][:, None] - peak.reshape(length >> level, 1 << level))
        numer = numer + (rescale[..., None] * stats[level][1][:, None, :]).reshape(length, width)
        denom = denom + (rescale * stats[level][2][:, None]).reshape(length)
    return numer / denom[:, None]

def reference(queries, keys, values, w_out, out_cotangent):
    tokens, channels = queries.shape
    heads = channels // HEAD_DIM

    def split_heads(field):
        return field.astype(jnp.float32).reshape(tokens, heads, HEAD_DIM).transpose(1, 0, 2)

    def join_heads(field):
        return field.transpose(1, 0, 2).reshape(tokens, channels).astype(jnp.bfloat16)
    one_head = jax.checkpoint(lambda triple: head_attention(triple[0], triple[1], triple[2]))

    def attend_all(query_all, key_all, value_all):
        return lax.map(one_head, (query_all, key_all, value_all))
    output, pull = jax.vjp(attend_all, split_heads(queries), split_heads(keys), split_heads(values))
    attn = join_heads(output)
    d_attn = lax.dot_general(out_cotangent, w_out, (((1,), (1,)), ((), ())), preferred_element_type=jnp.float32).astype(jnp.bfloat16)
    grads = pull(split_heads(d_attn))
    w_out_grad = lax.dot_general(out_cotangent, attn, (((0,), (0,)), ((), ())), preferred_element_type=jnp.float32) / math.sqrt(tokens)
    return (attn, join_heads(grads[0]), join_heads(grads[1]), join_heads(grads[2]), w_out_grad)
```

```python
import math

import jax
import jax.numpy as jnp
from jax import lax
from jax.sharding import Mesh, PartitionSpec as P

HEAD_DIM = 128
BLOCK = 128


highest = lax.Precision.HIGHEST


SEQ = ("sx", "sz")


def seq_size():
    return lax.psum(1, SEQ)


def partner_2(x, axis, bit):
    return lax.ppermute(x, axis, [(i, i ^ 1 << bit) for i in range(seq_size())])


def halve_units(field):
    count, units, width = field.shape
    return field.reshape(count, units // 2, 2, width).sum(2) * 0.5


def spread_units(field, factor):
    count, units, width = field.shape
    return jnp.broadcast_to(field[:, :, None, :] / factor, (count, units, factor, width)).reshape(
        count, units * factor, width
    )


def local_terms(query_units, key_units, value_units, level, scale):
    count, units, width = query_units.shape
    pairs = units // (2 * BLOCK)
    query_blocks = query_units.reshape(count, pairs, 2, BLOCK, width)
    key_blocks = key_units.reshape(count, pairs, 2 * BLOCK, width)
    value_blocks = value_units.reshape(count, pairs, 2 * BLOCK, width)
    scores = jnp.einsum("hpsqe,hpke->hpsqk", query_blocks, key_blocks, precision=highest) * scale
    top = jnp.max(scores, -1)
    weights = 2.0**level * jnp.exp(scores - top[..., None])
    numer = jnp.einsum("hpsqk,hpke->hpsqe", weights, value_blocks, precision=highest)
    saved = (query_blocks, key_blocks, value_blocks, weights)
    return (
        top.reshape(count, units),
        numer.reshape(count, units, width),
        weights.sum(-1).reshape(count, units),
        saved,
    )


def local_grads(saved, unit_out, unit_delta, scale):
    query_blocks, key_blocks, value_blocks, weights = saved
    count, pairs, _, block, width = query_blocks.shape
    units = pairs * 2 * block
    grad_blocks = unit_out.reshape(count, pairs, 2, block, width)
    delta_blocks = unit_delta.reshape(count, pairs, 2, block)
    inner = jnp.einsum("hpsqe,hpke->hpsqk", grad_blocks, value_blocks, precision=highest)
    dscore = weights * (inner - delta_blocks[..., None])
    dvalue = jnp.einsum("hpsqk,hpsqe->hpke", weights, grad_blocks, precision=highest)
    dquery = jnp.einsum("hpsqk,hpke->hpsqe", dscore, key_blocks, precision=highest) * scale
    dkey = jnp.einsum("hpsqk,hpsqe->hpke", dscore, query_blocks, precision=highest) * scale
    return (
        dquery.reshape(count, units, width),
        dkey.reshape(count, units, width),
        dvalue.reshape(count, units, width),
    )


def cross_terms(query_units, key_block, value_block, level, scale):
    scores = jnp.einsum("hqe,hke->hqk", query_units, key_block, precision=highest) * scale
    top = jnp.max(scores, -1)
    weights = 2.0**level * jnp.exp(scores - top[..., None])
    numer = jnp.einsum("hqk,hke->hqe", weights, value_block, precision=highest)
    return (top, numer, weights.sum(-1), weights)


def cross_grads(query_units, key_block, value_block, weights, unit_out, unit_delta, scale):
    inner = jnp.einsum("hqe,hke->hqk", unit_out, value_block, precision=highest)
    dscore = weights * (inner - unit_delta[..., None])
    dvalue = jnp.einsum("hqk,hqe->hke", weights, unit_out, precision=highest)
    dquery = jnp.einsum("hqk,hke->hqe", dscore, key_block, precision=highest) * scale
    dkey = jnp.einsum("hqk,hqe->hke", dscore, query_units, precision=highest) * scale
    return (dquery, dkey, dvalue)


def partner(blocks, bit):
    return partner_2((blocks[0], blocks[1]), SEQ, bit)


def partner_grads(blocks, bit):
    return partner_2((blocks[0], blocks[1]), SEQ, bit)


def per_device(queries, keys, values, w_out, out_cotangent):
    rows = queries.shape[0]
    heads = queries.shape[1] // HEAD_DIM
    scale = 1.0 / math.sqrt(HEAD_DIM)
    local = (rows // BLOCK).bit_length() - 1
    devices = seq_size()
    bits = devices.bit_length() - 1
    place = lax.axis_index(SEQ)

    def split_heads(field):
        return field.astype(jnp.float32).reshape(rows, heads, HEAD_DIM).transpose(1, 0, 2)

    def join_heads(field):
        return field.transpose(1, 0, 2).reshape(rows, heads * HEAD_DIM).astype(jnp.bfloat16)

    query_units = split_heads(queries)
    key_units = split_heads(keys)
    value_units = split_heads(values)
    tops = []
    numers = []
    denoms = []
    level = 0
    top, numer, denom, saved = local_terms(query_units, key_units, value_units, level, scale)
    tops.append(top)
    numers.append(numer)
    denoms.append(denom)
    local_saved = [saved]
    query_units = halve_units(query_units)
    key_units = halve_units(key_units)
    value_units = halve_units(value_units)
    own_keys = key_units
    own_values = value_units
    query_at = query_units
    far_saved = []
    for step in range(bits):
        if step > 0:
            query_at = halve_units(query_at)
            upper_side = place >> step - 1 & 1 == 1
            prior_keys = far_saved[-1][1]
            prior_values = far_saved[-1][2]
            own_keys = halve_units(
                jnp.concatenate(
                    [
                        jnp.where(upper_side, prior_keys, own_keys),
                        jnp.where(upper_side, own_keys, prior_keys),
                    ],
                    1,
                )
            )
            own_values = halve_units(
                jnp.concatenate(
                    [
                        jnp.where(upper_side, prior_values, own_values),
                        jnp.where(upper_side, own_values, prior_values),
                    ],
                    1,
                )
            )
        far_keys, far_values = partner((own_keys, own_values), step)
        top, numer, denom, weights = cross_terms(
            query_at, far_keys, far_values, local + step, scale
        )
        tops.append(top)
        numers.append(numer)
        denoms.append(denom)
        far_saved.append((query_at, far_keys, far_values, weights))
    count = local + bits
    peak = tops[0]
    for level in range(1, count):
        factor = 2**level
        peak = jnp.maximum(
            peak.reshape(heads, rows // factor, factor), tops[level][:, :, None]
        ).reshape(heads, rows)
    numer_sum = jnp.zeros((heads, rows, HEAD_DIM), jnp.float32)
    denom_sum = jnp.zeros((heads, rows), jnp.float32)
    for level in range(count):
        factor = 2**level
        rescale = jnp.exp(tops[level][:, :, None] - peak.reshape(heads, rows // factor, factor))
        numer_sum = numer_sum + (rescale[..., None] * numers[level][:, :, None, :]).reshape(
            heads, rows, HEAD_DIM
        )
        denom_sum = denom_sum + (rescale * denoms[level][:, :, None]).reshape(heads, rows)
    output = numer_sum / denom_sum[..., None]
    attn = join_heads(output)
    cotangent = lax.all_gather(out_cotangent, "heads", axis=1, tiled=True)
    d_attn = lax.dot_general(
        cotangent, w_out, (((1,), (1,)), ((), ())), preferred_element_type=jnp.float32
    ).astype(jnp.bfloat16)
    grad_out = split_heads(d_attn)
    delta = jnp.sum(grad_out * output, -1)
    query_acc = jnp.zeros((heads, rows, HEAD_DIM), jnp.float32)
    key_acc = jnp.zeros((heads, rows, HEAD_DIM), jnp.float32)
    value_acc = jnp.zeros((heads, rows, HEAD_DIM), jnp.float32)
    far_grads = []
    for level in range(count):
        factor = 2**level
        units = rows // factor
        share = jnp.exp(
            tops[level][:, :, None] - peak.reshape(heads, units, factor)
        ) / denom_sum.reshape(heads, units, factor)
        unit_out = (share[..., None] * grad_out.reshape(heads, units, factor, HEAD_DIM)).sum(2)
        unit_delta = (share * delta.reshape(heads, units, factor)).sum(2)
        if level < local:
            dquery, dkey, dvalue = local_grads(local_saved[level], unit_out, unit_delta, scale)
            key_acc = spread_units(dkey, factor)
            value_acc = spread_units(dvalue, factor)
        else:
            query_at, far_keys, far_values, weights = far_saved[level - local]
            dquery, dkey, dvalue = cross_grads(
                query_at, far_keys, far_values, weights, unit_out, unit_delta, scale
            )
            far_grads.append((dkey, dvalue))
        query_acc = query_acc + spread_units(dquery, factor)
    half = BLOCK // 2
    carry_keys = None
    carry_values = None
    for step in reversed(range(bits)):
        send_keys, send_values = far_grads[step]
        if carry_keys is not None:
            upper_side = place >> step & 1 == 1
            lower_keys = spread_units(carry_keys[:, :half], 2)
            upper_keys = spread_units(carry_keys[:, half:], 2)
            lower_values = spread_units(carry_values[:, :half], 2)
            upper_values = spread_units(carry_values[:, half:], 2)
            send_keys = send_keys + jnp.where(upper_side, lower_keys, upper_keys)
            send_values = send_values + jnp.where(upper_side, lower_values, upper_values)
            keep_keys = jnp.where(upper_side, upper_keys, lower_keys)
            keep_values = jnp.where(upper_side, upper_values, lower_values)
        else:
            keep_keys = jnp.zeros_like(send_keys)
            keep_values = jnp.zeros_like(send_values)
        got_keys, got_values = partner_grads((send_keys, send_values), step)
        carry_keys = keep_keys + got_keys
        carry_values = keep_values + got_values
    key_acc = key_acc + spread_units(carry_keys, 2**local)
    value_acc = value_acc + spread_units(carry_values, 2**local)
    norm = 1.0 / math.sqrt(rows * devices)
    outer = lax.psum(1, "sx")
    inner = lax.psum(1, "sz")
    features = cotangent.shape[1]
    block = features // (outer * inner)
    shuffled = cotangent.reshape(rows, outer, inner, block).transpose(0, 2, 1, 3).reshape(rows, features)
    partial = (
        lax.dot_general(
            shuffled, attn, (((0,), (0,)), ((), ())), preferred_element_type=jnp.float32
        )
        * norm
    )
    partial = lax.psum_scatter(partial, "sz", scatter_dimension=0, tiled=True)
    w_out_grad = lax.psum_scatter(partial, "sx", scatter_dimension=0, tiled=True)
    return (attn, join_heads(query_acc), join_heads(key_acc), join_heads(value_acc), w_out_grad)


def solution(mesh):
    in_specs = (
        P("seq", "heads"),
        P("seq", "heads"),
        P("seq", "heads"),
        P("heads", None),
        P("seq", "heads"),
    )
    out_specs = (
        P("seq", "heads"),
        P("seq", "heads"),
        P("seq", "heads"),
        P("seq", "heads"),
        P("seq", "heads"),
    )
    zs = sorted({d.coords[2] for d in mesh.devices[:, 0]}) if hasattr(mesh.devices[0, 0], "coords") else [0] * 8
    inner = len(zs) if mesh.shape["seq"] % len(zs) == 0 else 1
    grid = Mesh(mesh.devices.reshape(mesh.shape["seq"] // inner, inner, mesh.shape["heads"]), ("sx", "sz", "heads"))
    in_specs = tuple(P(*[SEQ if a == "seq" else a for a in spec]) for spec in in_specs)
    out_specs = tuple(P(*[SEQ if a == "seq" else a for a in spec]) for spec in out_specs)
    return jax.shard_map(
        per_device, mesh=grid, in_specs=in_specs, out_specs=out_specs, check_vma=False
    )
```

```python
import math

import jax
import jax.numpy as jnp
from jax import lax
from jax.sharding import Mesh, PartitionSpec as P

HEAD_DIM = 128
BLOCK = 128


highest = lax.Precision.HIGHEST


SEQ = ("sx", "sz")


def seq_size():
    return lax.psum(1, SEQ)


def partner_2(x, axis, bit):
    return lax.ppermute(x, axis, [(i, i ^ 1 << bit) for i in range(seq_size())])


def halve_units(field):
    count, units, width = field.shape
    return field.reshape(count, units // 2, 2, width).sum(2) * 0.5


def spread_units(field, factor):
    count, units, width = field.shape
    return jnp.broadcast_to(field[:, :, None, :] / factor, (count, units, factor, width)).reshape(
        count, units * factor, width
    )


def local_terms(query_units, key_units, value_units, level, scale):
    count, units, width = query_units.shape
    pairs = units // (2 * BLOCK)
    query_blocks = query_units.reshape(count, pairs, 2, BLOCK, width)
    key_blocks = key_units.reshape(count, pairs, 2 * BLOCK, width)
    value_blocks = value_units.reshape(count, pairs, 2 * BLOCK, width)
    scores = jnp.einsum("hpsqe,hpke->hpsqk", query_blocks, key_blocks, precision=highest) * scale
    top = jnp.max(scores, -1)
    weights = 2.0**level * jnp.exp(scores - top[..., None])
    numer = jnp.einsum("hpsqk,hpke->hpsqe", weights, value_blocks, precision=highest)
    saved = (query_blocks, key_blocks, value_blocks, weights)
    return (
        top.reshape(count, units),
        numer.reshape(count, units, width),
        weights.sum(-1).reshape(count, units),
        saved,
    )


def local_grads(saved, unit_out, unit_delta, scale):
    query_blocks, key_blocks, value_blocks, weights = saved
    count, pairs, _, block, width = query_blocks.shape
    units = pairs * 2 * block
    grad_blocks = unit_out.reshape(count, pairs, 2, block, width)
    delta_blocks = unit_delta.reshape(count, pairs, 2, block)
    inner = jnp.einsum("hpsqe,hpke->hpsqk", grad_blocks, value_blocks, precision=highest)
    dscore = weights * (inner - delta_blocks[..., None])
    dvalue = jnp.einsum("hpsqk,hpsqe->hpke", weights, grad_blocks, precision=highest)
    dquery = jnp.einsum("hpsqk,hpke->hpsqe", dscore, key_blocks, precision=highest) * scale
    dkey = jnp.einsum("hpsqk,hpsqe->hpke", dscore, query_blocks, precision=highest) * scale
    return (
        dquery.reshape(count, units, width),
        dkey.reshape(count, units, width),
        dvalue.reshape(count, units, width),
    )


def cross_terms(query_units, key_block, value_block, level, scale):
    scores = jnp.einsum("hqe,hke->hqk", query_units, key_block, precision=highest) * scale
    top = jnp.max(scores, -1)
    weights = 2.0**level * jnp.exp(scores - top[..., None])
    numer = jnp.einsum("hqk,hke->hqe", weights, value_block, precision=highest)
    return (top, numer, weights.sum(-1), weights)


def cross_grads(query_units, key_block, value_block, weights, unit_out, unit_delta, scale):
    inner = jnp.einsum("hqe,hke->hqk", unit_out, value_block, precision=highest)
    dscore = weights * (inner - unit_delta[..., None])
    dvalue = jnp.einsum("hqk,hqe->hke", weights, unit_out, precision=highest)
    dquery = jnp.einsum("hqk,hke->hqe", dscore, key_block, precision=highest) * scale
    dkey = jnp.einsum("hqk,hqe->hke", dscore, query_units, precision=highest) * scale
    return (dquery, dkey, dvalue)


def partner(blocks, bit):
    return partner_2((blocks[0], blocks[1]), SEQ, bit)


def partner_grads(blocks, bit):
    return partner_2((blocks[0], blocks[1]), SEQ, bit)


def per_device(queries, keys, values, w_out, out_cotangent):
    rows = queries.shape[0]
    heads = queries.shape[1] // HEAD_DIM
    scale = 1.0 / math.sqrt(HEAD_DIM)
    local = (rows // BLOCK).bit_length() - 1
    devices = seq_size()
    bits = devices.bit_length() - 1
    place = lax.axis_index(SEQ)

    def split_heads(field):
        return field.astype(jnp.float32).reshape(rows, heads, HEAD_DIM).transpose(1, 0, 2)

    def join_heads(field):
        return field.transpose(1, 0, 2).reshape(rows, heads * HEAD_DIM).astype(jnp.bfloat16)

    assert local == 1
    query_units = split_heads(queries)
    key_units = split_heads(keys)
    value_units = split_heads(values)
    level_queries = [query_units]
    far_keys_all = []
    far_values_all = []
    query_at = halve_units(query_units)
    own_keys = halve_units(key_units)
    own_values = halve_units(value_units)
    for step in range(bits):
        if step > 0:
            query_at = halve_units(query_at)
            upper_side = place >> step - 1 & 1 == 1
            prior_keys = far_keys_all[-1]
            prior_values = far_values_all[-1]
            own_keys = halve_units(
                jnp.concatenate(
                    [
                        jnp.where(upper_side, prior_keys, own_keys),
                        jnp.where(upper_side, own_keys, prior_keys),
                    ],
                    1,
                )
            )
            own_values = halve_units(
                jnp.concatenate(
                    [
                        jnp.where(upper_side, prior_values, own_values),
                        jnp.where(upper_side, own_values, prior_values),
                    ],
                    1,
                )
            )
        far_keys, far_values = partner((own_keys, own_values), step)
        level_queries.append(query_at)
        far_keys_all.append(far_keys)
        far_values_all.append(far_values)
    count = local + bits
    segments = [jnp.einsum("hqe,hke->hqk", query_units, key_units, precision=highest) * scale]
    gains = [jnp.ones((rows,), jnp.float32)]
    for level in range(1, count):
        unit_scores = (
            jnp.einsum(
                "hqe,hke->hqk", level_queries[level], far_keys_all[level - 1], precision=highest
            )
            * scale
        )
        segments.append(jnp.repeat(unit_scores, 2**level, axis=1))
        gains.append(jnp.full((BLOCK,), 2.0**level, jnp.float32))
    scores = jnp.concatenate(segments, -1)
    peak = jnp.max(scores, -1, keepdims=True)
    weights = jnp.concatenate(gains)[None, None, :] * jnp.exp(scores - peak)
    denom_sum = weights.sum(-1, keepdims=True)
    all_values = jnp.concatenate([value_units] + far_values_all, 1)
    numer_sum = jnp.einsum("hqk,hke->hqe", weights, all_values, precision=highest)
    output = numer_sum / denom_sum
    attn = join_heads(output)
    cotangent = lax.all_gather(out_cotangent, "heads", axis=1, tiled=True)
    d_attn = lax.dot_general(
        cotangent, w_out, (((1,), (1,)), ((), ())), preferred_element_type=jnp.float32
    ).astype(jnp.bfloat16)
    grad_out = split_heads(d_attn)
    delta = jnp.sum(grad_out * output, -1, keepdims=True)
    probs = weights / denom_sum
    inner = jnp.einsum("hqe,hke->hqk", grad_out, all_values, precision=highest)
    dscore = probs * (inner - delta)
    dvalue_all = jnp.einsum("hqk,hqe->hke", probs, grad_out, precision=highest)
    local_dscore = dscore[:, :, :rows]
    query_acc = jnp.einsum("hqk,hke->hqe", local_dscore, key_units, precision=highest) * scale
    key_acc = jnp.einsum("hqk,hqe->hke", local_dscore, query_units, precision=highest) * scale
    value_acc = dvalue_all[:, :rows]
    far_grads = []
    for level in range(1, count):
        factor = 2**level
        start = rows + (level - 1) * BLOCK
        unit_dscore = (
            dscore[:, :, start : start + BLOCK]
            .reshape(heads, rows // factor, factor, BLOCK)
            .sum(2)
        )
        dquery = (
            jnp.einsum(
                "hqk,hke->hqe", unit_dscore, far_keys_all[level - 1], precision=highest
            )
            * scale
        )
        dkey = (
            jnp.einsum("hqk,hqe->hke", unit_dscore, level_queries[level], precision=highest)
            * scale
        )
        far_grads.append((dkey, dvalue_all[:, start : start + BLOCK]))
        query_acc = query_acc + spread_units(dquery, factor)
    half = BLOCK // 2
    carry_keys = None
    carry_values = None
    for step in reversed(range(bits)):
        send_keys, send_values = far_grads[step]
        if carry_keys is not None:
            upper_side = place >> step & 1 == 1
            lower_keys = spread_units(carry_keys[:, :half], 2)
            upper_keys = spread_units(carry_keys[:, half:], 2)
            lower_values = spread_units(carry_values[:, :half], 2)
            upper_values = spread_units(carry_values[:, half:], 2)
            send_keys = send_keys + jnp.where(upper_side, lower_keys, upper_keys)
            send_values = send_values + jnp.where(upper_side, lower_values, upper_values)
            keep_keys = jnp.where(upper_side, upper_keys, lower_keys)
            keep_values = jnp.where(upper_side, upper_values, lower_values)
        else:
            keep_keys = jnp.zeros_like(send_keys)
            keep_values = jnp.zeros_like(send_values)
        got_keys, got_values = partner_grads((send_keys, send_values), step)
        carry_keys = keep_keys + got_keys
        carry_values = keep_values + got_values
    key_acc = key_acc + spread_units(carry_keys, 2**local)
    value_acc = value_acc + spread_units(carry_values, 2**local)
    norm = 1.0 / math.sqrt(rows * devices)
    outer = lax.psum(1, "sx")
    inner = lax.psum(1, "sz")
    features = cotangent.shape[1]
    block = features // (outer * inner)
    shuffled = cotangent.reshape(rows, outer, inner, block).transpose(0, 2, 1, 3).reshape(rows, features)
    partial = (
        lax.dot_general(
            shuffled, attn, (((0,), (0,)), ((), ())), preferred_element_type=jnp.float32
        )
        * norm
    )
    partial = lax.psum_scatter(partial, "sz", scatter_dimension=0, tiled=True)
    w_out_grad = lax.psum_scatter(partial, "sx", scatter_dimension=0, tiled=True)
    return (attn, join_heads(query_acc), join_heads(key_acc), join_heads(value_acc), w_out_grad)


def solution(mesh):
    in_specs = (
        P("seq", "heads"),
        P("seq", "heads"),
        P("seq", "heads"),
        P("heads", None),
        P("seq", "heads"),
    )
    out_specs = (
        P("seq", "heads"),
        P("seq", "heads"),
        P("seq", "heads"),
        P("seq", "heads"),
        P("seq", "heads"),
    )
    zs = sorted({d.coords[2] for d in mesh.devices[:, 0]}) if hasattr(mesh.devices[0, 0], "coords") else [0] * 8
    inner = len(zs) if mesh.shape["seq"] % len(zs) == 0 else 1
    grid = Mesh(mesh.devices.reshape(mesh.shape["seq"] // inner, inner, mesh.shape["heads"]), ("sx", "sz", "heads"))
    in_specs = tuple(P(*[SEQ if a == "seq" else a for a in spec]) for spec in in_specs)
    out_specs = tuple(P(*[SEQ if a == "seq" else a for a in spec]) for spec in out_specs)
    return jax.shard_map(
        per_device, mesh=grid, in_specs=in_specs, out_specs=out_specs, check_vma=False
    )
```

```python
import math

import jax
import jax.numpy as jnp
from jax import lax
from jax.sharding import Mesh, PartitionSpec as P

HEAD_DIM = 128
BLOCK = 128


highest = lax.Precision.HIGHEST


SEQ = ("sx", "sz")


def seq_size():
    return lax.psum(1, SEQ)


def partner_2(x, axis, bit):
    return lax.ppermute(x, axis, [(i, i ^ 1 << bit) for i in range(seq_size())])


def sibling_pairs(level, shift, devices):
    low = level - 1
    return [(d, ((d >> low ^ 1) << low) | ((d & (1 << low) - 1) ^ shift)) for d in range(devices)]


def halve_units(field):
    count, units, width = field.shape
    return field.reshape(count, units // 2, 2, width).sum(2) * 0.5


def spread_units(field, factor):
    count, units, width = field.shape
    return jnp.broadcast_to(field[:, :, None, :] / factor, (count, units, factor, width)).reshape(
        count, units * factor, width
    )


def local_terms(query_units, key_units, value_units, level, scale):
    count, units, width = query_units.shape
    pairs = units // (2 * BLOCK)
    query_blocks = query_units.reshape(count, pairs, 2, BLOCK, width)
    key_blocks = key_units.reshape(count, pairs, 2 * BLOCK, width)
    value_blocks = value_units.reshape(count, pairs, 2 * BLOCK, width)
    scores = jnp.einsum("hpsqe,hpke->hpsqk", query_blocks, key_blocks, precision=highest) * scale
    top = jnp.max(scores, -1)
    weights = 2.0**level * jnp.exp(scores - top[..., None])
    numer = jnp.einsum("hpsqk,hpke->hpsqe", weights, value_blocks, precision=highest)
    saved = (query_blocks, key_blocks, value_blocks, weights)
    return (
        top.reshape(count, units),
        numer.reshape(count, units, width),
        weights.sum(-1).reshape(count, units),
        saved,
    )


def local_grads(saved, unit_out, unit_delta, scale):
    query_blocks, key_blocks, value_blocks, weights = saved
    count, pairs, _, block, width = query_blocks.shape
    units = pairs * 2 * block
    grad_blocks = unit_out.reshape(count, pairs, 2, block, width)
    delta_blocks = unit_delta.reshape(count, pairs, 2, block)
    inner = jnp.einsum("hpsqe,hpke->hpsqk", grad_blocks, value_blocks, precision=highest)
    dscore = weights * (inner - delta_blocks[..., None])
    dvalue = jnp.einsum("hpsqk,hpsqe->hpke", weights, grad_blocks, precision=highest)
    dquery = jnp.einsum("hpsqk,hpke->hpsqe", dscore, key_blocks, precision=highest) * scale
    dkey = jnp.einsum("hpsqk,hpsqe->hpke", dscore, query_blocks, precision=highest) * scale
    return (
        dquery.reshape(count, units, width),
        dkey.reshape(count, units, width),
        dvalue.reshape(count, units, width),
    )


def cross_terms(query_units, key_block, value_block, level, scale):
    scores = jnp.einsum("hqe,hke->hqk", query_units, key_block, precision=highest) * scale
    top = jnp.max(scores, -1)
    weights = 2.0**level * jnp.exp(scores - top[..., None])
    numer = jnp.einsum("hqk,hke->hqe", weights, value_block, precision=highest)
    return (top, numer, weights.sum(-1), weights)


def cross_grads(query_units, key_block, value_block, weights, unit_out, unit_delta, scale):
    inner = jnp.einsum("hqe,hke->hqk", unit_out, value_block, precision=highest)
    dscore = weights * (inner - unit_delta[..., None])
    dvalue = jnp.einsum("hqk,hqe->hke", weights, unit_out, precision=highest)
    dquery = jnp.einsum("hqk,hke->hqe", dscore, key_block, precision=highest) * scale
    dkey = jnp.einsum("hqk,hqe->hke", dscore, query_units, precision=highest) * scale
    return (dquery, dkey, dvalue)


def partner(blocks, bit):
    return partner_2((blocks[0], blocks[1]), SEQ, bit)


def partner_grads(blocks, bit):
    return partner_2((blocks[0], blocks[1]), SEQ, bit)


def per_device(queries, keys, values, w_out, out_cotangent):
    rows = queries.shape[0]
    heads = queries.shape[1] // HEAD_DIM
    scale = 1.0 / math.sqrt(HEAD_DIM)
    local = (rows // BLOCK).bit_length() - 1
    devices = seq_size()
    bits = devices.bit_length() - 1
    place = lax.axis_index(SEQ)

    def split_heads(field):
        return field.astype(jnp.float32).reshape(rows, heads, HEAD_DIM).transpose(1, 0, 2)

    def join_heads(field):
        return field.transpose(1, 0, 2).reshape(rows, heads * HEAD_DIM).astype(jnp.bfloat16)

    assert local == 1
    query_units = split_heads(queries)
    key_units = split_heads(keys)
    value_units = split_heads(values)
    level_queries = [query_units]
    far_keys_all = []
    far_values_all = []
    query_at, own_keys, own_values = query_units, key_units, value_units
    for level in range(1, bits + 1):
        query_at = halve_units(query_at)
        own_keys = halve_units(own_keys)
        own_values = halve_units(own_values)
        level_queries.append(query_at)
        units = rows >> level
        packed = jnp.concatenate([own_keys, own_values], 1)
        pieces = [
            lax.ppermute(packed, SEQ, sibling_pairs(level, shift, devices))
            for shift in range(1 << level - 1)
        ]
        far_keys_all.append(jnp.concatenate([piece[:, :units] for piece in pieces], 1))
        far_values_all.append(jnp.concatenate([piece[:, units:] for piece in pieces], 1))
    count = local + bits
    segments = [jnp.einsum("hqe,hke->hqk", query_units, key_units, precision=highest) * scale]
    gains = [jnp.ones((rows,), jnp.float32)]
    for level in range(1, count):
        unit_scores = (
            jnp.einsum(
                "hqe,hke->hqk", level_queries[level], far_keys_all[level - 1], precision=highest
            )
            * scale
        )
        segments.append(jnp.repeat(unit_scores, 2**level, axis=1))
        gains.append(jnp.full((BLOCK,), 2.0**level, jnp.float32))
    scores = jnp.concatenate(segments, -1)
    peak = jnp.max(scores, -1, keepdims=True)
    weights = jnp.concatenate(gains)[None, None, :] * jnp.exp(scores - peak)
    denom_sum = weights.sum(-1, keepdims=True)
    all_values = jnp.concatenate([value_units] + far_values_all, 1)
    numer_sum = jnp.einsum("hqk,hke->hqe", weights, all_values, precision=highest)
    output = numer_sum / denom_sum
    attn = join_heads(output)
    cotangent = lax.all_gather(out_cotangent, "heads", axis=1, tiled=True)
    d_attn = lax.dot_general(
        cotangent, w_out, (((1,), (1,)), ((), ())), preferred_element_type=jnp.float32
    ).astype(jnp.bfloat16)
    grad_out = split_heads(d_attn)
    delta = jnp.sum(grad_out * output, -1, keepdims=True)
    probs = weights / denom_sum
    inner = jnp.einsum("hqe,hke->hqk", grad_out, all_values, precision=highest)
    dscore = probs * (inner - delta)
    dvalue_all = jnp.einsum("hqk,hqe->hke", probs, grad_out, precision=highest)
    local_dscore = dscore[:, :, :rows]
    query_acc = jnp.einsum("hqk,hke->hqe", local_dscore, key_units, precision=highest) * scale
    key_acc = jnp.einsum("hqk,hqe->hke", local_dscore, query_units, precision=highest) * scale
    value_acc = dvalue_all[:, :rows]
    far_grads = []
    for level in range(1, count):
        factor = 2**level
        start = rows + (level - 1) * BLOCK
        unit_dscore = (
            dscore[:, :, start : start + BLOCK]
            .reshape(heads, rows // factor, factor, BLOCK)
            .sum(2)
        )
        dquery = (
            jnp.einsum(
                "hqk,hke->hqe", unit_dscore, far_keys_all[level - 1], precision=highest
            )
            * scale
        )
        dkey = (
            jnp.einsum("hqk,hqe->hke", unit_dscore, level_queries[level], precision=highest)
            * scale
        )
        dvalue = dvalue_all[:, start : start + BLOCK]
        units = rows >> level
        returned = None
        for shift in range(1 << level - 1):
            piece = jnp.concatenate(
                [
                    dkey[:, shift * units : (shift + 1) * units],
                    dvalue[:, shift * units : (shift + 1) * units],
                ],
                1,
            )
            got = lax.ppermute(piece, SEQ, sibling_pairs(level, shift, devices))
            returned = got if returned is None else returned + got
        key_acc = key_acc + spread_units(returned[:, :units], factor)
        value_acc = value_acc + spread_units(returned[:, units:], factor)
        query_acc = query_acc + spread_units(dquery, factor)
    norm = 1.0 / math.sqrt(rows * devices)
    outer = lax.psum(1, "sx")
    inner = lax.psum(1, "sz")
    features = cotangent.shape[1]
    block = features // (outer * inner)
    shuffled = cotangent.reshape(rows, outer, inner, block).transpose(0, 2, 1, 3).reshape(rows, features)
    partial = (
        lax.dot_general(
            shuffled, attn, (((0,), (0,)), ((), ())), preferred_element_type=jnp.float32
        )
        * norm
    )
    partial = lax.psum_scatter(partial, "sz", scatter_dimension=0, tiled=True)
    w_out_grad = lax.psum_scatter(partial, "sx", scatter_dimension=0, tiled=True)
    return (attn, join_heads(query_acc), join_heads(key_acc), join_heads(value_acc), w_out_grad)


def solution(mesh):
    in_specs = (
        P("seq", "heads"),
        P("seq", "heads"),
        P("seq", "heads"),
        P("heads", None),
        P("seq", "heads"),
    )
    out_specs = (
        P("seq", "heads"),
        P("seq", "heads"),
        P("seq", "heads"),
        P("seq", "heads"),
        P("seq", "heads"),
    )
    zs = sorted({d.coords[2] for d in mesh.devices[:, 0]}) if hasattr(mesh.devices[0, 0], "coords") else [0] * 8
    inner = len(zs) if mesh.shape["seq"] % len(zs) == 0 else 1
    grid = Mesh(mesh.devices.reshape(mesh.shape["seq"] // inner, inner, mesh.shape["heads"]), ("sx", "sz", "heads"))
    in_specs = tuple(P(*[SEQ if a == "seq" else a for a in spec]) for spec in in_specs)
    out_specs = tuple(P(*[SEQ if a == "seq" else a for a in spec]) for spec in out_specs)
    return jax.shard_map(
        per_device, mesh=grid, in_specs=in_specs, out_specs=out_specs, check_vma=False
    )
```

```python
import math

import jax
import jax.numpy as jnp
from jax import lax
from jax.sharding import Mesh, PartitionSpec as P

HEAD_DIM = 128
BLOCK = 128


highest = lax.Precision.HIGHEST


SEQ = ("sx", "sz")


def seq_size():
    return lax.psum(1, SEQ)


def partner_2(x, axis, bit):
    return lax.ppermute(x, axis, [(i, i ^ 1 << bit) for i in range(seq_size())])


def halve_units(field):
    count, units, width = field.shape
    return field.reshape(count, units // 2, 2, width).sum(2) * 0.5


def spread_units(field, factor):
    count, units, width = field.shape
    return jnp.broadcast_to(field[:, :, None, :] / factor, (count, units, factor, width)).reshape(
        count, units * factor, width
    )


def local_terms(query_units, key_units, value_units, level, scale):
    count, units, width = query_units.shape
    pairs = units // (2 * BLOCK)
    query_blocks = query_units.reshape(count, pairs, 2, BLOCK, width)
    key_blocks = key_units.reshape(count, pairs, 2 * BLOCK, width)
    value_blocks = value_units.reshape(count, pairs, 2 * BLOCK, width)
    scores = jnp.einsum("hpsqe,hpke->hpsqk", query_blocks, key_blocks, precision=highest) * scale
    top = jnp.max(scores, -1)
    weights = 2.0**level * jnp.exp(scores - top[..., None])
    numer = jnp.einsum("hpsqk,hpke->hpsqe", weights, value_blocks, precision=highest)
    saved = (query_blocks, key_blocks, value_blocks, weights)
    return (
        top.reshape(count, units),
        numer.reshape(count, units, width),
        weights.sum(-1).reshape(count, units),
        saved,
    )


def local_grads(saved, unit_out, unit_delta, scale):
    query_blocks, key_blocks, value_blocks, weights = saved
    count, pairs, _, block, width = query_blocks.shape
    units = pairs * 2 * block
    grad_blocks = unit_out.reshape(count, pairs, 2, block, width)
    delta_blocks = unit_delta.reshape(count, pairs, 2, block)
    inner = jnp.einsum("hpsqe,hpke->hpsqk", grad_blocks, value_blocks, precision=highest)
    dscore = weights * (inner - delta_blocks[..., None])
    dvalue = jnp.einsum("hpsqk,hpsqe->hpke", weights, grad_blocks, precision=highest)
    dquery = jnp.einsum("hpsqk,hpke->hpsqe", dscore, key_blocks, precision=highest) * scale
    dkey = jnp.einsum("hpsqk,hpsqe->hpke", dscore, query_blocks, precision=highest) * scale
    return (
        dquery.reshape(count, units, width),
        dkey.reshape(count, units, width),
        dvalue.reshape(count, units, width),
    )


def cross_terms(query_units, key_block, value_block, level, scale):
    scores = jnp.einsum("hqe,hke->hqk", query_units, key_block, precision=highest) * scale
    top = jnp.max(scores, -1)
    weights = 2.0**level * jnp.exp(scores - top[..., None])
    numer = jnp.einsum("hqk,hke->hqe", weights, value_block, precision=highest)
    return (top, numer, weights.sum(-1), weights)


def cross_grads(query_units, key_block, value_block, weights, unit_out, unit_delta, scale):
    inner = jnp.einsum("hqe,hke->hqk", unit_out, value_block, precision=highest)
    dscore = weights * (inner - unit_delta[..., None])
    dvalue = jnp.einsum("hqk,hqe->hke", weights, unit_out, precision=highest)
    dquery = jnp.einsum("hqk,hke->hqe", dscore, key_block, precision=highest) * scale
    dkey = jnp.einsum("hqk,hqe->hke", dscore, query_units, precision=highest) * scale
    return (dquery, dkey, dvalue)


def partner(blocks, bit):
    units = blocks[0].shape[1]
    both = partner_2(jnp.concatenate(blocks, 1), SEQ, bit)
    return both[:, :units], both[:, units:]


def partner_grads(blocks, bit):
    return partner(blocks, bit)


def per_device(queries, keys, values, w_out, out_cotangent):
    rows = queries.shape[0]
    heads = queries.shape[1] // HEAD_DIM
    scale = 1.0 / math.sqrt(HEAD_DIM)
    local = (rows // BLOCK).bit_length() - 1
    devices = seq_size()
    bits = devices.bit_length() - 1
    place = lax.axis_index(SEQ)

    def split_heads(field):
        return field.astype(jnp.float32).reshape(rows, heads, HEAD_DIM).transpose(1, 0, 2)

    def join_heads(field):
        return field.transpose(1, 0, 2).reshape(rows, heads * HEAD_DIM).astype(jnp.bfloat16)

    assert local == 1
    query_units = split_heads(queries)
    key_units = split_heads(keys)
    value_units = split_heads(values)
    level_queries = [query_units]
    far_keys_all = []
    far_values_all = []
    query_at = halve_units(query_units)
    own_keys = halve_units(key_units)
    own_values = halve_units(value_units)
    for step in range(bits):
        if step > 0:
            query_at = halve_units(query_at)
            upper_side = place >> step - 1 & 1 == 1
            prior_keys = far_keys_all[-1]
            prior_values = far_values_all[-1]
            own_keys = halve_units(
                jnp.concatenate(
                    [
                        jnp.where(upper_side, prior_keys, own_keys),
                        jnp.where(upper_side, own_keys, prior_keys),
                    ],
                    1,
                )
            )
            own_values = halve_units(
                jnp.concatenate(
                    [
                        jnp.where(upper_side, prior_values, own_values),
                        jnp.where(upper_side, own_values, prior_values),
                    ],
                    1,
                )
            )
        far_keys, far_values = partner((own_keys, own_values), step)
        level_queries.append(query_at)
        far_keys_all.append(far_keys)
        far_values_all.append(far_values)
    count = local + bits
    segments = [jnp.einsum("hqe,hke->hqk", query_units, key_units, precision=highest) * scale]
    gains = [jnp.ones((rows,), jnp.float32)]
    for level in range(1, count):
        unit_scores = (
            jnp.einsum(
                "hqe,hke->hqk", level_queries[level], far_keys_all[level - 1], precision=highest
            )
            * scale
        )
        segments.append(jnp.repeat(unit_scores, 2**level, axis=1))
        gains.append(jnp.full((BLOCK,), 2.0**level, jnp.float32))
    scores = jnp.concatenate(segments, -1)
    peak = jnp.max(scores, -1, keepdims=True)
    weights = jnp.concatenate(gains)[None, None, :] * jnp.exp(scores - peak)
    denom_sum = weights.sum(-1, keepdims=True)
    all_values = jnp.concatenate([value_units] + far_values_all, 1)
    numer_sum = jnp.einsum("hqk,hke->hqe", weights, all_values, precision=highest)
    output = numer_sum / denom_sum
    attn = join_heads(output)
    cotangent = lax.all_gather(out_cotangent, "heads", axis=1, tiled=True)
    d_attn = lax.dot_general(
        cotangent, w_out, (((1,), (1,)), ((), ())), preferred_element_type=jnp.float32
    ).astype(jnp.bfloat16)
    grad_out = split_heads(d_attn)
    delta = jnp.sum(grad_out * output, -1, keepdims=True)
    probs = weights / denom_sum
    inner = jnp.einsum("hqe,hke->hqk", grad_out, all_values, precision=highest)
    dscore = probs * (inner - delta)
    dvalue_all = jnp.einsum("hqk,hqe->hke", probs, grad_out, precision=highest)
    local_dscore = dscore[:, :, :rows]
    query_acc = jnp.einsum("hqk,hke->hqe", local_dscore, key_units, precision=highest) * scale
    key_acc = jnp.einsum("hqk,hqe->hke", local_dscore, query_units, precision=highest) * scale
    value_acc = dvalue_all[:, :rows]
    far_grads = []
    for level in range(1, count):
        factor = 2**level
        start = rows + (level - 1) * BLOCK
        unit_dscore = (
            dscore[:, :, start : start + BLOCK]
            .reshape(heads, rows // factor, factor, BLOCK)
            .sum(2)
        )
        dquery = (
            jnp.einsum(
                "hqk,hke->hqe", unit_dscore, far_keys_all[level - 1], precision=highest
            )
            * scale
        )
        dkey = (
            jnp.einsum("hqk,hqe->hke", unit_dscore, level_queries[level], precision=highest)
            * scale
        )
        far_grads.append((dkey, dvalue_all[:, start : start + BLOCK]))
        query_acc = query_acc + spread_units(dquery, factor)
    half = BLOCK // 2
    carry_keys = None
    carry_values = None
    for step in reversed(range(bits)):
        send_keys, send_values = far_grads[step]
        if carry_keys is not None:
            upper_side = place >> step & 1 == 1
            lower_keys = spread_units(carry_keys[:, :half], 2)
            upper_keys = spread_units(carry_keys[:, half:], 2)
            lower_values = spread_units(carry_values[:, :half], 2)
            upper_values = spread_units(carry_values[:, half:], 2)
            send_keys = send_keys + jnp.where(upper_side, lower_keys, upper_keys)
            send_values = send_values + jnp.where(upper_side, lower_values, upper_values)
            keep_keys = jnp.where(upper_side, upper_keys, lower_keys)
            keep_values = jnp.where(upper_side, upper_values, lower_values)
        else:
            keep_keys = jnp.zeros_like(send_keys)
            keep_values = jnp.zeros_like(send_values)
        got_keys, got_values = partner_grads((send_keys, send_values), step)
        carry_keys = keep_keys + got_keys
        carry_values = keep_values + got_values
    key_acc = key_acc + spread_units(carry_keys, 2**local)
    value_acc = value_acc + spread_units(carry_values, 2**local)
    norm = 1.0 / math.sqrt(rows * devices)
    outer = lax.psum(1, "sx")
    inner = lax.psum(1, "sz")
    features = cotangent.shape[1]
    block = features // (outer * inner)
    shuffled = cotangent.reshape(rows, outer, inner, block).transpose(0, 2, 1, 3).reshape(rows, features)
    partial = (
        lax.dot_general(
            shuffled, attn, (((0,), (0,)), ((), ())), preferred_element_type=jnp.float32
        )
        * norm
    )
    partial = lax.psum_scatter(partial, "sz", scatter_dimension=0, tiled=True)
    w_out_grad = lax.psum_scatter(partial, "sx", scatter_dimension=0, tiled=True)
    return (attn, join_heads(query_acc), join_heads(key_acc), join_heads(value_acc), w_out_grad)


def solution(mesh):
    in_specs = (
        P("seq", "heads"),
        P("seq", "heads"),
        P("seq", "heads"),
        P("heads", None),
        P("seq", "heads"),
    )
    out_specs = (
        P("seq", "heads"),
        P("seq", "heads"),
        P("seq", "heads"),
        P("seq", "heads"),
        P("seq", "heads"),
    )
    zs = sorted({d.coords[2] for d in mesh.devices[:, 0]}) if hasattr(mesh.devices[0, 0], "coords") else [0] * 8
    inner = len(zs) if mesh.shape["seq"] % len(zs) == 0 else 1
    grid = Mesh(mesh.devices.reshape(mesh.shape["seq"] // inner, inner, mesh.shape["heads"]), ("sx", "sz", "heads"))
    in_specs = tuple(P(*[SEQ if a == "seq" else a for a in spec]) for spec in in_specs)
    out_specs = tuple(P(*[SEQ if a == "seq" else a for a in spec]) for spec in out_specs)
    return jax.shard_map(
        per_device, mesh=grid, in_specs=in_specs, out_specs=out_specs, check_vma=False
    )
```

```python
import math

import jax
import jax.numpy as jnp
from jax import lax
from jax.sharding import Mesh, PartitionSpec as P

HEAD_DIM = 128
BLOCK = 128


highest = lax.Precision.HIGHEST


SEQ = ("sx", "sz")


def seq_size():
    return lax.psum(1, SEQ)


def partner_2(x, axis, bit):
    return lax.ppermute(x, axis, [(i, i ^ 1 << bit) for i in range(seq_size())])


def halve_units(field):
    count, units, width = field.shape
    return field.reshape(count, units // 2, 2, width).sum(2) * 0.5


def spread_units(field, factor):
    count, units, width = field.shape
    return jnp.broadcast_to(field[:, :, None, :] / factor, (count, units, factor, width)).reshape(
        count, units * factor, width
    )


def local_terms(query_units, key_units, value_units, level, scale):
    count, units, width = query_units.shape
    pairs = units // (2 * BLOCK)
    query_blocks = query_units.reshape(count, pairs, 2, BLOCK, width)
    key_blocks = key_units.reshape(count, pairs, 2 * BLOCK, width)
    value_blocks = value_units.reshape(count, pairs, 2 * BLOCK, width)
    scores = jnp.einsum("hpsqe,hpke->hpsqk", query_blocks, key_blocks, precision=highest) * scale
    top = jnp.max(scores, -1)
    weights = 2.0**level * jnp.exp(scores - top[..., None])
    numer = jnp.einsum("hpsqk,hpke->hpsqe", weights, value_blocks, precision=highest)
    saved = (query_blocks, key_blocks, value_blocks, weights)
    return (
        top.reshape(count, units),
        numer.reshape(count, units, width),
        weights.sum(-1).reshape(count, units),
        saved,
    )


def local_grads(saved, unit_out, unit_delta, scale):
    query_blocks, key_blocks, value_blocks, weights = saved
    count, pairs, _, block, width = query_blocks.shape
    units = pairs * 2 * block
    grad_blocks = unit_out.reshape(count, pairs, 2, block, width)
    delta_blocks = unit_delta.reshape(count, pairs, 2, block)
    inner = jnp.einsum("hpsqe,hpke->hpsqk", grad_blocks, value_blocks, precision=highest)
    dscore = weights * (inner - delta_blocks[..., None])
    dvalue = jnp.einsum("hpsqk,hpsqe->hpke", weights, grad_blocks, precision=highest)
    dquery = jnp.einsum("hpsqk,hpke->hpsqe", dscore, key_blocks, precision=highest) * scale
    dkey = jnp.einsum("hpsqk,hpsqe->hpke", dscore, query_blocks, precision=highest) * scale
    return (
        dquery.reshape(count, units, width),
        dkey.reshape(count, units, width),
        dvalue.reshape(count, units, width),
    )


def cross_terms(query_units, key_block, value_block, level, scale):
    scores = jnp.einsum("hqe,hke->hqk", query_units, key_block, precision=highest) * scale
    top = jnp.max(scores, -1)
    weights = 2.0**level * jnp.exp(scores - top[..., None])
    numer = jnp.einsum("hqk,hke->hqe", weights, value_block, precision=highest)
    return (top, numer, weights.sum(-1), weights)


def cross_grads(query_units, key_block, value_block, weights, unit_out, unit_delta, scale):
    inner = jnp.einsum("hqe,hke->hqk", unit_out, value_block, precision=highest)
    dscore = weights * (inner - unit_delta[..., None])
    dvalue = jnp.einsum("hqk,hqe->hke", weights, unit_out, precision=highest)
    dquery = jnp.einsum("hqk,hke->hqe", dscore, key_block, precision=highest) * scale
    dkey = jnp.einsum("hqk,hqe->hke", dscore, query_units, precision=highest) * scale
    return (dquery, dkey, dvalue)


def partner(blocks, bit):
    units = blocks[0].shape[1]
    both = partner_2(jnp.concatenate(blocks, 1), SEQ, bit)
    return both[:, :units], both[:, units:]


def partner_grads(blocks, bit):
    return partner(blocks, bit)


def per_device(queries, keys, values, w_out, out_cotangent):
    rows = queries.shape[0]
    heads = queries.shape[1] // HEAD_DIM
    scale = 1.0 / math.sqrt(HEAD_DIM)
    local = (rows // BLOCK).bit_length() - 1
    devices = seq_size()
    bits = devices.bit_length() - 1
    place = lax.axis_index(SEQ)

    def split_heads(field):
        return field.astype(jnp.float32).reshape(rows, heads, HEAD_DIM).transpose(1, 0, 2)

    def join_heads(field):
        return field.transpose(1, 0, 2).reshape(rows, heads * HEAD_DIM).astype(jnp.bfloat16)

    assert local == 1
    query_units = split_heads(queries)
    key_units = split_heads(keys)
    value_units = split_heads(values)
    level_queries = [query_units]
    far_keys_all = []
    far_values_all = []
    query_at = halve_units(query_units)
    own_keys = halve_units(key_units)
    own_values = halve_units(value_units)
    for step in range(bits):
        if step > 0:
            query_at = halve_units(query_at)
            upper_side = place >> step - 1 & 1 == 1
            prior_keys = far_keys_all[-1]
            prior_values = far_values_all[-1]
            own_keys = halve_units(
                jnp.concatenate(
                    [
                        jnp.where(upper_side, prior_keys, own_keys),
                        jnp.where(upper_side, own_keys, prior_keys),
                    ],
                    1,
                )
            )
            own_values = halve_units(
                jnp.concatenate(
                    [
                        jnp.where(upper_side, prior_values, own_values),
                        jnp.where(upper_side, own_values, prior_values),
                    ],
                    1,
                )
            )
        far_keys, far_values = partner((own_keys, own_values), step)
        level_queries.append(query_at)
        far_keys_all.append(far_keys)
        far_values_all.append(far_values)
    count = local + bits
    segments = [jnp.einsum("hqe,hke->hqk", query_units, key_units, precision=highest) * scale]
    gains = [jnp.ones((rows,), jnp.float32)]
    for level in range(1, count):
        unit_scores = (
            jnp.einsum(
                "hqe,hke->hqk", level_queries[level], far_keys_all[level - 1], precision=highest
            )
            * scale
        )
        segments.append(jnp.repeat(unit_scores, 2**level, axis=1))
        gains.append(jnp.full((BLOCK,), 2.0**level, jnp.float32))
    scores = jnp.concatenate(segments, -1)
    peak = jnp.max(scores, -1, keepdims=True)
    weights = jnp.concatenate(gains)[None, None, :] * jnp.exp(scores - peak)
    denom_sum = weights.sum(-1, keepdims=True)
    all_values = jnp.concatenate([value_units] + far_values_all, 1)
    numer_sum = jnp.einsum("hqk,hke->hqe", weights, all_values, precision=highest)
    output = numer_sum / denom_sum
    attn = join_heads(output)
    cotangent = lax.all_gather(out_cotangent, "heads", axis=1, tiled=True)
    d_attn = lax.dot_general(
        cotangent, w_out, (((1,), (1,)), ((), ())), preferred_element_type=jnp.float32
    ).astype(jnp.bfloat16)
    grad_out = split_heads(d_attn)
    delta = jnp.sum(grad_out * output, -1, keepdims=True)
    probs = weights / denom_sum
    inner = jnp.einsum("hqe,hke->hqk", grad_out, all_values, precision=highest)
    dscore = probs * (inner - delta)
    dvalue_all = jnp.einsum("hqk,hqe->hke", probs, grad_out, precision=highest)
    local_dscore = dscore[:, :, :rows]
    query_acc = jnp.einsum("hqk,hke->hqe", local_dscore, key_units, precision=highest) * scale
    key_acc = jnp.einsum("hqk,hqe->hke", local_dscore, query_units, precision=highest) * scale
    value_acc = dvalue_all[:, :rows]
    far_grads = []
    for level in range(1, count):
        factor = 2**level
        start = rows + (level - 1) * BLOCK
        unit_dscore = (
            dscore[:, :, start : start + BLOCK]
            .reshape(heads, rows // factor, factor, BLOCK)
            .sum(2)
        )
        dquery = (
            jnp.einsum(
                "hqk,hke->hqe", unit_dscore, far_keys_all[level - 1], precision=highest
            )
            * scale
        )
        dkey = (
            jnp.einsum("hqk,hqe->hke", unit_dscore, level_queries[level], precision=highest)
            * scale
        )
        far_grads.append((dkey, dvalue_all[:, start : start + BLOCK]))
        query_acc = query_acc + spread_units(dquery, factor)
    half = BLOCK // 2
    carry_keys = None
    carry_values = None
    for step in reversed(range(bits)):
        send_keys, send_values = far_grads[step]
        if carry_keys is not None:
            upper_side = place >> step & 1 == 1
            lower_keys = spread_units(carry_keys[:, :half], 2)
            upper_keys = spread_units(carry_keys[:, half:], 2)
            lower_values = spread_units(carry_values[:, :half], 2)
            upper_values = spread_units(carry_values[:, half:], 2)
            send_keys = send_keys + jnp.where(upper_side, lower_keys, upper_keys)
            send_values = send_values + jnp.where(upper_side, lower_values, upper_values)
            keep_keys = jnp.where(upper_side, upper_keys, lower_keys)
            keep_values = jnp.where(upper_side, upper_values, lower_values)
        else:
            keep_keys = jnp.zeros_like(send_keys)
            keep_values = jnp.zeros_like(send_values)
        got_keys, got_values = partner_grads((send_keys, send_values), step)
        carry_keys = keep_keys + got_keys
        carry_values = keep_values + got_values
    key_acc = key_acc + spread_units(carry_keys, 2**local)
    value_acc = value_acc + spread_units(carry_values, 2**local)
    norm = 1.0 / math.sqrt(rows * devices)
    partial = (
        lax.dot_general(
            cotangent, attn, (((0,), (0,)), ((), ())), preferred_element_type=jnp.float32
        )
        * norm
    )
    partial = lax.psum_scatter(partial, "sx", scatter_dimension=0, tiled=True)
    w_out_grad = lax.psum_scatter(partial, "sz", scatter_dimension=0, tiled=True)
    return (attn, join_heads(query_acc), join_heads(key_acc), join_heads(value_acc), w_out_grad)


def solution(mesh):
    in_specs = (
        P("seq", "heads"),
        P("seq", "heads"),
        P("seq", "heads"),
        P("heads", None),
        P("seq", "heads"),
    )
    out_specs = (
        P("seq", "heads"),
        P("seq", "heads"),
        P("seq", "heads"),
        P("seq", "heads"),
        P("seq", "heads"),
    )
    zs = sorted({d.coords[2] for d in mesh.devices[:, 0]}) if hasattr(mesh.devices[0, 0], "coords") else [0] * 8
    inner = len(zs) if mesh.shape["seq"] % len(zs) == 0 else 1
    grid = Mesh(mesh.devices.reshape(mesh.shape["seq"] // inner, inner, mesh.shape["heads"]), ("sx", "sz", "heads"))
    in_specs = tuple(P(*[SEQ if a == "seq" else a for a in spec]) for spec in in_specs)
    out_specs = tuple(P(*[SEQ if a == "seq" else a for a in spec]) for spec in out_specs)
    return jax.shard_map(
        per_device, mesh=grid, in_specs=in_specs, out_specs=out_specs, check_vma=False
    )
```

```python
import math

import jax
import jax.numpy as jnp
from jax import lax
from jax.sharding import Mesh, PartitionSpec as P

HEAD_DIM = 128
BLOCK = 128


highest = lax.Precision.HIGHEST


SEQ = ("sx", "sz")


def seq_size():
    return lax.psum(1, SEQ)


def partner_2(x, axis, bit):
    return lax.ppermute(x, axis, [(i, i ^ 1 << bit) for i in range(seq_size())])


def halve_units(field):
    count, units, width = field.shape
    return field.reshape(count, units // 2, 2, width).sum(2) * 0.5


def spread_units(field, factor):
    count, units, width = field.shape
    return jnp.broadcast_to(field[:, :, None, :] / factor, (count, units, factor, width)).reshape(
        count, units * factor, width
    )


def local_terms(query_units, key_units, value_units, level, scale):
    count, units, width = query_units.shape
    pairs = units // (2 * BLOCK)
    query_blocks = query_units.reshape(count, pairs, 2, BLOCK, width)
    key_blocks = key_units.reshape(count, pairs, 2 * BLOCK, width)
    value_blocks = value_units.reshape(count, pairs, 2 * BLOCK, width)
    scores = jnp.einsum("hpsqe,hpke->hpsqk", query_blocks, key_blocks, precision=highest) * scale
    top = jnp.max(scores, -1)
    weights = 2.0**level * jnp.exp(scores - top[..., None])
    numer = jnp.einsum("hpsqk,hpke->hpsqe", weights, value_blocks, precision=highest)
    saved = (query_blocks, key_blocks, value_blocks, weights)
    return (
        top.reshape(count, units),
        numer.reshape(count, units, width),
        weights.sum(-1).reshape(count, units),
        saved,
    )


def local_grads(saved, unit_out, unit_delta, scale):
    query_blocks, key_blocks, value_blocks, weights = saved
    count, pairs, _, block, width = query_blocks.shape
    units = pairs * 2 * block
    grad_blocks = unit_out.reshape(count, pairs, 2, block, width)
    delta_blocks = unit_delta.reshape(count, pairs, 2, block)
    inner = jnp.einsum("hpsqe,hpke->hpsqk", grad_blocks, value_blocks, precision=highest)
    dscore = weights * (inner - delta_blocks[..., None])
    dvalue = jnp.einsum("hpsqk,hpsqe->hpke", weights, grad_blocks, precision=highest)
    dquery = jnp.einsum("hpsqk,hpke->hpsqe", dscore, key_blocks, precision=highest) * scale
    dkey = jnp.einsum("hpsqk,hpsqe->hpke", dscore, query_blocks, precision=highest) * scale
    return (
        dquery.reshape(count, units, width),
        dkey.reshape(count, units, width),
        dvalue.reshape(count, units, width),
    )


def cross_terms(query_units, key_block, value_block, level, scale):
    scores = jnp.einsum("hqe,hke->hqk", query_units, key_block, precision=highest) * scale
    top = jnp.max(scores, -1)
    weights = 2.0**level * jnp.exp(scores - top[..., None])
    numer = jnp.einsum("hqk,hke->hqe", weights, value_block, precision=highest)
    return (top, numer, weights.sum(-1), weights)


def cross_grads(query_units, key_block, value_block, weights, unit_out, unit_delta, scale):
    inner = jnp.einsum("hqe,hke->hqk", unit_out, value_block, precision=highest)
    dscore = weights * (inner - unit_delta[..., None])
    dvalue = jnp.einsum("hqk,hqe->hke", weights, unit_out, precision=highest)
    dquery = jnp.einsum("hqk,hke->hqe", dscore, key_block, precision=highest) * scale
    dkey = jnp.einsum("hqk,hqe->hke", dscore, query_units, precision=highest) * scale
    return (dquery, dkey, dvalue)


def partner(blocks, bit):
    units = blocks[0].shape[1]
    both = partner_2(jnp.concatenate(blocks, 1), SEQ, bit)
    return both[:, :units], both[:, units:]


def partner_grads(blocks, bit):
    return partner(blocks, bit)


def per_device(queries, keys, values, w_out, out_cotangent):
    rows = queries.shape[0]
    heads = queries.shape[1] // HEAD_DIM
    scale = 1.0 / math.sqrt(HEAD_DIM)
    local = (rows // BLOCK).bit_length() - 1
    devices = seq_size()
    bits = devices.bit_length() - 1
    place = lax.axis_index(SEQ)

    def split_heads(field):
        return field.astype(jnp.float32).reshape(rows, heads, HEAD_DIM).transpose(1, 0, 2)

    def join_heads(field):
        return field.transpose(1, 0, 2).reshape(rows, heads * HEAD_DIM).astype(jnp.bfloat16)

    assert local == 1
    query_units = split_heads(queries)
    key_units = split_heads(keys)
    value_units = split_heads(values)
    level_queries = [query_units]
    far_keys_all = []
    far_values_all = []
    query_at = halve_units(query_units)
    own = halve_units(jnp.concatenate([key_units, value_units], 1))
    half = BLOCK // 2
    for step in range(bits):
        if step > 0:
            query_at = halve_units(query_at)
            upper_side = place >> step - 1 & 1 == 1
            lower = halve_units(jnp.where(upper_side, far, own))
            upper = halve_units(jnp.where(upper_side, own, far))
            own = jnp.concatenate(
                [lower[:, :half], upper[:, :half], lower[:, half:], upper[:, half:]], 1
            )
        far = partner_2(own, SEQ, step)
        level_queries.append(query_at)
        far_keys_all.append(far[:, :BLOCK])
        far_values_all.append(far[:, BLOCK:])
    count = local + bits
    segments = [jnp.einsum("hqe,hke->hqk", query_units, key_units, precision=highest) * scale]
    gains = [jnp.ones((rows,), jnp.float32)]
    for level in range(1, count):
        unit_scores = (
            jnp.einsum(
                "hqe,hke->hqk", level_queries[level], far_keys_all[level - 1], precision=highest
            )
            * scale
        )
        segments.append(jnp.repeat(unit_scores, 2**level, axis=1))
        gains.append(jnp.full((BLOCK,), 2.0**level, jnp.float32))
    scores = jnp.concatenate(segments, -1)
    peak = jnp.max(scores, -1, keepdims=True)
    weights = jnp.concatenate(gains)[None, None, :] * jnp.exp(scores - peak)
    denom_sum = weights.sum(-1, keepdims=True)
    all_values = jnp.concatenate([value_units] + far_values_all, 1)
    numer_sum = jnp.einsum("hqk,hke->hqe", weights, all_values, precision=highest)
    output = numer_sum / denom_sum
    attn = join_heads(output)
    cotangent = lax.all_gather(out_cotangent, "heads", axis=1, tiled=True)
    d_attn = lax.dot_general(
        cotangent, w_out, (((1,), (1,)), ((), ())), preferred_element_type=jnp.float32
    ).astype(jnp.bfloat16)
    grad_out = split_heads(d_attn)
    delta = jnp.sum(grad_out * output, -1, keepdims=True)
    probs = weights / denom_sum
    inner = jnp.einsum("hqe,hke->hqk", grad_out, all_values, precision=highest)
    dscore = probs * (inner - delta)
    dvalue_all = jnp.einsum("hqk,hqe->hke", probs, grad_out, precision=highest)
    local_dscore = dscore[:, :, :rows]
    query_acc = jnp.einsum("hqk,hke->hqe", local_dscore, key_units, precision=highest) * scale
    key_acc = jnp.einsum("hqk,hqe->hke", local_dscore, query_units, precision=highest) * scale
    value_acc = dvalue_all[:, :rows]
    far_grads = []
    for level in range(1, count):
        factor = 2**level
        start = rows + (level - 1) * BLOCK
        unit_dscore = (
            dscore[:, :, start : start + BLOCK]
            .reshape(heads, rows // factor, factor, BLOCK)
            .sum(2)
        )
        dquery = (
            jnp.einsum(
                "hqk,hke->hqe", unit_dscore, far_keys_all[level - 1], precision=highest
            )
            * scale
        )
        dkey = (
            jnp.einsum("hqk,hqe->hke", unit_dscore, level_queries[level], precision=highest)
            * scale
        )
        far_grads.append((dkey, dvalue_all[:, start : start + BLOCK]))
        query_acc = query_acc + spread_units(dquery, factor)
    carry = None
    for step in reversed(range(bits)):
        send = jnp.concatenate(far_grads[step], 1)
        if carry is not None:
            upper_side = place >> step & 1 == 1
            lower = spread_units(jnp.concatenate([carry[:, :half], carry[:, BLOCK : BLOCK + half]], 1), 2)
            upper = spread_units(jnp.concatenate([carry[:, half:BLOCK], carry[:, BLOCK + half :]], 1), 2)
            send = send + jnp.where(upper_side, lower, upper)
            keep = jnp.where(upper_side, upper, lower)
        else:
            keep = jnp.zeros_like(send)
        carry = keep + partner_2(send, SEQ, step)
    key_acc = key_acc + spread_units(carry[:, :BLOCK], 2**local)
    value_acc = value_acc + spread_units(carry[:, BLOCK:], 2**local)
    norm = 1.0 / math.sqrt(rows * devices)
    outer = lax.psum(1, "sx")
    inner = lax.psum(1, "sz")
    features = cotangent.shape[1]
    block = features // (outer * inner)
    shuffled = cotangent.reshape(rows, outer, inner, block).transpose(0, 2, 1, 3).reshape(rows, features)
    partial = (
        lax.dot_general(
            shuffled, attn, (((0,), (0,)), ((), ())), preferred_element_type=jnp.float32
        )
        * norm
    )
    partial = lax.psum_scatter(partial, "sz", scatter_dimension=0, tiled=True)
    w_out_grad = lax.psum_scatter(partial, "sx", scatter_dimension=0, tiled=True)
    return (attn, join_heads(query_acc), join_heads(key_acc), join_heads(value_acc), w_out_grad)


def solution(mesh):
    in_specs = (
        P("seq", "heads"),
        P("seq", "heads"),
        P("seq", "heads"),
        P("heads", None),
        P("seq", "heads"),
    )
    out_specs = (
        P("seq", "heads"),
        P("seq", "heads"),
        P("seq", "heads"),
        P("seq", "heads"),
        P("seq", "heads"),
    )
    zs = sorted({d.coords[2] for d in mesh.devices[:, 0]}) if hasattr(mesh.devices[0, 0], "coords") else [0] * 8
    inner = len(zs) if mesh.shape["seq"] % len(zs) == 0 else 1
    grid = Mesh(mesh.devices.reshape(mesh.shape["seq"] // inner, inner, mesh.shape["heads"]), ("sx", "sz", "heads"))
    in_specs = tuple(P(*[SEQ if a == "seq" else a for a in spec]) for spec in in_specs)
    out_specs = tuple(P(*[SEQ if a == "seq" else a for a in spec]) for spec in out_specs)
    return jax.shard_map(
        per_device, mesh=grid, in_specs=in_specs, out_specs=out_specs, check_vma=False
    )
```

```python
import math

import jax
import jax.numpy as jnp
from jax import lax
from jax.sharding import Mesh, PartitionSpec as P

HEAD_DIM = 128
BLOCK = 128


highest = lax.Precision.HIGHEST


SEQ = ("sx", "sz")


def seq_size():
    return lax.psum(1, SEQ)


def partner_2(x, axis, bit):
    return lax.ppermute(x, axis, [(i, i ^ 1 << bit) for i in range(seq_size())])


def halve_units(field):
    count, units, width = field.shape
    return field.reshape(count, units // 2, 2, width).sum(2) * 0.5


def spread_units(field, factor):
    count, units, width = field.shape
    return jnp.broadcast_to(field[:, :, None, :] / factor, (count, units, factor, width)).reshape(
        count, units * factor, width
    )


def local_terms(query_units, key_units, value_units, level, scale):
    count, units, width = query_units.shape
    pairs = units // (2 * BLOCK)
    query_blocks = query_units.reshape(count, pairs, 2, BLOCK, width)
    key_blocks = key_units.reshape(count, pairs, 2 * BLOCK, width)
    value_blocks = value_units.reshape(count, pairs, 2 * BLOCK, width)
    scores = jnp.einsum("hpsqe,hpke->hpsqk", query_blocks, key_blocks, precision=highest) * scale
    top = jnp.max(scores, -1)
    weights = 2.0**level * jnp.exp(scores - top[..., None])
    numer = jnp.einsum("hpsqk,hpke->hpsqe", weights, value_blocks, precision=highest)
    saved = (query_blocks, key_blocks, value_blocks, weights)
    return (
        top.reshape(count, units),
        numer.reshape(count, units, width),
        weights.sum(-1).reshape(count, units),
        saved,
    )


def local_grads(saved, unit_out, unit_delta, scale):
    query_blocks, key_blocks, value_blocks, weights = saved
    count, pairs, _, block, width = query_blocks.shape
    units = pairs * 2 * block
    grad_blocks = unit_out.reshape(count, pairs, 2, block, width)
    delta_blocks = unit_delta.reshape(count, pairs, 2, block)
    inner = jnp.einsum("hpsqe,hpke->hpsqk", grad_blocks, value_blocks, precision=highest)
    dscore = weights * (inner - delta_blocks[..., None])
    dvalue = jnp.einsum("hpsqk,hpsqe->hpke", weights, grad_blocks, precision=highest)
    dquery = jnp.einsum("hpsqk,hpke->hpsqe", dscore, key_blocks, precision=highest) * scale
    dkey = jnp.einsum("hpsqk,hpsqe->hpke", dscore, query_blocks, precision=highest) * scale
    return (
        dquery.reshape(count, units, width),
        dkey.reshape(count, units, width),
        dvalue.reshape(count, units, width),
    )


def cross_terms(query_units, key_block, value_block, level, scale):
    scores = jnp.einsum("hqe,hke->hqk", query_units, key_block, precision=highest) * scale
    top = jnp.max(scores, -1)
    weights = 2.0**level * jnp.exp(scores - top[..., None])
    numer = jnp.einsum("hqk,hke->hqe", weights, value_block, precision=highest)
    return (top, numer, weights.sum(-1), weights)


def cross_grads(query_units, key_block, value_block, weights, unit_out, unit_delta, scale):
    inner = jnp.einsum("hqe,hke->hqk", unit_out, value_block, precision=highest)
    dscore = weights * (inner - unit_delta[..., None])
    dvalue = jnp.einsum("hqk,hqe->hke", weights, unit_out, precision=highest)
    dquery = jnp.einsum("hqk,hke->hqe", dscore, key_block, precision=highest) * scale
    dkey = jnp.einsum("hqk,hqe->hke", dscore, query_units, precision=highest) * scale
    return (dquery, dkey, dvalue)


def partner(blocks, bit):
    units = blocks[0].shape[1]
    both = partner_2(jnp.concatenate(blocks, 1), SEQ, bit)
    return both[:, :units], both[:, units:]


def partner_grads(blocks, bit):
    return partner(blocks, bit)


def per_device(queries, keys, values, w_out, out_cotangent):
    rows = queries.shape[0]
    heads = queries.shape[1] // HEAD_DIM
    scale = 1.0 / math.sqrt(HEAD_DIM)
    local = (rows // BLOCK).bit_length() - 1
    devices = seq_size()
    bits = devices.bit_length() - 1
    place = lax.axis_index(SEQ)

    def split_heads(field):
        return field.astype(jnp.float32).reshape(rows, heads, HEAD_DIM).transpose(1, 0, 2)

    def join_heads(field):
        return field.transpose(1, 0, 2).reshape(rows, heads * HEAD_DIM).astype(jnp.bfloat16)

    assert local == 1
    query_units = split_heads(queries)
    key_units = split_heads(keys)
    value_units = split_heads(values)
    level_queries = [query_units]
    far_keys_all = []
    far_values_all = []
    query_at = halve_units(query_units)
    own = halve_units(jnp.concatenate([key_units, value_units], 1))
    half = BLOCK // 2
    for step in range(bits):
        if step > 0:
            query_at = halve_units(query_at)
            upper_side = place >> step - 1 & 1 == 1
            lower = halve_units(jnp.where(upper_side, far, own))
            upper = halve_units(jnp.where(upper_side, own, far))
            own = jnp.concatenate(
                [lower[:, :half], upper[:, :half], lower[:, half:], upper[:, half:]], 1
            )
        far = partner_2(own, SEQ, step)
        level_queries.append(query_at)
        far_keys_all.append(far[:, :BLOCK])
        far_values_all.append(far[:, BLOCK:])
    count = local + bits
    segments = [jnp.einsum("hqe,hke->hqk", query_units, key_units, precision=highest) * scale]
    gains = [jnp.ones((rows,), jnp.float32)]
    for level in range(1, count):
        unit_scores = (
            jnp.einsum(
                "hqe,hke->hqk", level_queries[level], far_keys_all[level - 1], precision=highest
            )
            * scale
        )
        segments.append(jnp.repeat(unit_scores, 2**level, axis=1))
        gains.append(jnp.full((BLOCK,), 2.0**level, jnp.float32))
    scores = jnp.concatenate(segments, -1)
    peak = jnp.max(scores, -1, keepdims=True)
    weights = jnp.concatenate(gains)[None, None, :] * jnp.exp(scores - peak)
    denom_sum = weights.sum(-1, keepdims=True)
    all_values = jnp.concatenate([value_units] + far_values_all, 1)
    numer_sum = jnp.einsum("hqk,hke->hqe", weights, all_values, precision=highest)
    output = numer_sum / denom_sum
    attn = join_heads(output)
    cotangent = lax.all_gather(out_cotangent, "heads", axis=1, tiled=True)
    d_attn = lax.dot_general(
        cotangent, w_out, (((1,), (1,)), ((), ())), preferred_element_type=jnp.float32
    ).astype(jnp.bfloat16)
    grad_out = split_heads(d_attn)
    delta = jnp.sum(grad_out * output, -1, keepdims=True)
    probs = weights / denom_sum
    inner = jnp.einsum("hqe,hke->hqk", grad_out, all_values, precision=highest)
    dscore = probs * (inner - delta)
    dvalue_all = jnp.einsum("hqk,hqe->hke", probs, grad_out, precision=highest)
    local_dscore = dscore[:, :, :rows]
    query_acc = jnp.einsum("hqk,hke->hqe", local_dscore, key_units, precision=highest) * scale
    key_acc = jnp.einsum("hqk,hqe->hke", local_dscore, query_units, precision=highest) * scale
    value_acc = dvalue_all[:, :rows]
    far_grads = []
    for level in range(1, count):
        factor = 2**level
        start = rows + (level - 1) * BLOCK
        unit_dscore = (
            dscore[:, :, start : start + BLOCK]
            .reshape(heads, rows // factor, factor, BLOCK)
            .sum(2)
        )
        dquery = (
            jnp.einsum(
                "hqk,hke->hqe", unit_dscore, far_keys_all[level - 1], precision=highest
            )
            * scale
        )
        dkey = (
            jnp.einsum("hqk,hqe->hke", unit_dscore, level_queries[level], precision=highest)
            * scale
        )
        far_grads.append((dkey, dvalue_all[:, start : start + BLOCK]))
        query_acc = query_acc + spread_units(dquery, factor)
    carry = None
    for step in reversed(range(bits)):
        send = jnp.concatenate(far_grads[step], 1)
        if carry is not None:
            upper_side = place >> step & 1 == 1
            lower = spread_units(jnp.concatenate([carry[:, :half], carry[:, BLOCK : BLOCK + half]], 1), 2)
            upper = spread_units(jnp.concatenate([carry[:, half:BLOCK], carry[:, BLOCK + half :]], 1), 2)
            send = send + jnp.where(upper_side, lower, upper)
            keep = jnp.where(upper_side, upper, lower)
        else:
            keep = jnp.zeros_like(send)
        carry = keep + partner_2(send, SEQ, step)
    key_acc = key_acc + spread_units(carry[:, :BLOCK], 2**local)
    value_acc = value_acc + spread_units(carry[:, BLOCK:], 2**local)
    norm = 1.0 / math.sqrt(rows * devices)
    outer = lax.psum(1, "sx")
    inner = lax.psum(1, "sz")
    features = cotangent.shape[1]
    block = features // (outer * inner)
    shuffled = cotangent.reshape(rows, outer, inner, block).transpose(0, 2, 1, 3).reshape(rows, features)
    split = attn.shape[1] // 2
    first = (
        lax.dot_general(
            shuffled, attn[:, :split], (((0,), (0,)), ((), ())), preferred_element_type=jnp.float32
        )
        * norm
    )
    second = (
        lax.dot_general(
            cotangent, attn[:, split:], (((0,), (0,)), ((), ())), preferred_element_type=jnp.float32
        )
        * norm
    )
    first = lax.psum_scatter(first, "sz", scatter_dimension=0, tiled=True)
    second = lax.psum_scatter(second, "sx", scatter_dimension=0, tiled=True)
    first = lax.psum_scatter(first, "sx", scatter_dimension=0, tiled=True)
    second = lax.psum_scatter(second, "sz", scatter_dimension=0, tiled=True)
    w_out_grad = jnp.concatenate([first, second], 1)
    return (attn, join_heads(query_acc), join_heads(key_acc), join_heads(value_acc), w_out_grad)


def solution(mesh):
    in_specs = (
        P("seq", "heads"),
        P("seq", "heads"),
        P("seq", "heads"),
        P("heads", None),
        P("seq", "heads"),
    )
    out_specs = (
        P("seq", "heads"),
        P("seq", "heads"),
        P("seq", "heads"),
        P("seq", "heads"),
        P("seq", "heads"),
    )
    zs = sorted({d.coords[2] for d in mesh.devices[:, 0]}) if hasattr(mesh.devices[0, 0], "coords") else [0] * 8
    inner = len(zs) if mesh.shape["seq"] % len(zs) == 0 else 1
    grid = Mesh(mesh.devices.reshape(mesh.shape["seq"] // inner, inner, mesh.shape["heads"]), ("sx", "sz", "heads"))
    in_specs = tuple(P(*[SEQ if a == "seq" else a for a in spec]) for spec in in_specs)
    out_specs = tuple(P(*[SEQ if a == "seq" else a for a in spec]) for spec in out_specs)
    return jax.shard_map(
        per_device, mesh=grid, in_specs=in_specs, out_specs=out_specs, check_vma=False
    )
```

```python
import math

import jax
import jax.numpy as jnp
from jax import lax
from jax.sharding import Mesh, PartitionSpec as P

HEAD_DIM = 128
BLOCK = 128


highest = lax.Precision.HIGHEST


SEQ = ("sx", "sz")


def seq_size():
    return lax.psum(1, SEQ)


def partner_2(x, axis, bit):
    return lax.ppermute(x, axis, [(i, i ^ 1 << bit) for i in range(seq_size())])


def halve_units(field):
    count, units, width = field.shape
    return field.reshape(count, units // 2, 2, width).sum(2) * 0.5


def spread_units(field, factor):
    count, units, width = field.shape
    return jnp.broadcast_to(field[:, :, None, :] / factor, (count, units, factor, width)).reshape(
        count, units * factor, width
    )


def local_terms(query_units, key_units, value_units, level, scale):
    count, units, width = query_units.shape
    pairs = units // (2 * BLOCK)
    query_blocks = query_units.reshape(count, pairs, 2, BLOCK, width)
    key_blocks = key_units.reshape(count, pairs, 2 * BLOCK, width)
    value_blocks = value_units.reshape(count, pairs, 2 * BLOCK, width)
    scores = jnp.einsum("hpsqe,hpke->hpsqk", query_blocks, key_blocks, precision=highest) * scale
    top = jnp.max(scores, -1)
    weights = 2.0**level * jnp.exp(scores - top[..., None])
    numer = jnp.einsum("hpsqk,hpke->hpsqe", weights, value_blocks, precision=highest)
    saved = (query_blocks, key_blocks, value_blocks, weights)
    return (
        top.reshape(count, units),
        numer.reshape(count, units, width),
        weights.sum(-1).reshape(count, units),
        saved,
    )


def local_grads(saved, unit_out, unit_delta, scale):
    query_blocks, key_blocks, value_blocks, weights = saved
    count, pairs, _, block, width = query_blocks.shape
    units = pairs * 2 * block
    grad_blocks = unit_out.reshape(count, pairs, 2, block, width)
    delta_blocks = unit_delta.reshape(count, pairs, 2, block)
    inner = jnp.einsum("hpsqe,hpke->hpsqk", grad_blocks, value_blocks, precision=highest)
    dscore = weights * (inner - delta_blocks[..., None])
    dvalue = jnp.einsum("hpsqk,hpsqe->hpke", weights, grad_blocks, precision=highest)
    dquery = jnp.einsum("hpsqk,hpke->hpsqe", dscore, key_blocks, precision=highest) * scale
    dkey = jnp.einsum("hpsqk,hpsqe->hpke", dscore, query_blocks, precision=highest) * scale
    return (
        dquery.reshape(count, units, width),
        dkey.reshape(count, units, width),
        dvalue.reshape(count, units, width),
    )


def cross_terms(query_units, key_block, value_block, level, scale):
    scores = jnp.einsum("hqe,hke->hqk", query_units, key_block, precision=highest) * scale
    top = jnp.max(scores, -1)
    weights = 2.0**level * jnp.exp(scores - top[..., None])
    numer = jnp.einsum("hqk,hke->hqe", weights, value_block, precision=highest)
    return (top, numer, weights.sum(-1), weights)


def cross_grads(query_units, key_block, value_block, weights, unit_out, unit_delta, scale):
    inner = jnp.einsum("hqe,hke->hqk", unit_out, value_block, precision=highest)
    dscore = weights * (inner - unit_delta[..., None])
    dvalue = jnp.einsum("hqk,hqe->hke", weights, unit_out, precision=highest)
    dquery = jnp.einsum("hqk,hke->hqe", dscore, key_block, precision=highest) * scale
    dkey = jnp.einsum("hqk,hqe->hke", dscore, query_units, precision=highest) * scale
    return (dquery, dkey, dvalue)


def partner(blocks, bit):
    units = blocks[0].shape[1]
    both = partner_2(jnp.concatenate(blocks, 1), SEQ, bit)
    return both[:, :units], both[:, units:]


def partner_grads(blocks, bit):
    return partner(blocks, bit)


def per_device(queries, keys, values, w_out, out_cotangent):
    rows = queries.shape[0]
    heads = queries.shape[1] // HEAD_DIM
    scale = 1.0 / math.sqrt(HEAD_DIM)
    local = (rows // BLOCK).bit_length() - 1
    devices = seq_size()
    bits = devices.bit_length() - 1
    place = lax.axis_index(SEQ)

    def split_heads(field):
        return field.astype(jnp.float32).reshape(rows, heads, HEAD_DIM).transpose(1, 0, 2)

    def join_heads(field):
        return field.transpose(1, 0, 2).reshape(rows, heads * HEAD_DIM).astype(jnp.bfloat16)

    assert local == 1
    query_units = split_heads(queries)
    key_units = split_heads(keys)
    value_units = split_heads(values)
    level_queries = [query_units]
    far_keys_all = []
    far_values_all = []
    query_at = halve_units(query_units)
    own = halve_units(jnp.concatenate([key_units, value_units], 1))
    half = BLOCK // 2
    for step in range(bits):
        if step > 0:
            query_at = halve_units(query_at)
            upper_side = place >> step - 1 & 1 == 1
            lower = halve_units(jnp.where(upper_side, far, own))
            upper = halve_units(jnp.where(upper_side, own, far))
            own = jnp.concatenate(
                [lower[:, :half], upper[:, :half], lower[:, half:], upper[:, half:]], 1
            )
        far = partner_2(own, SEQ, step)
        level_queries.append(query_at)
        far_keys_all.append(far[:, :BLOCK])
        far_values_all.append(far[:, BLOCK:])
    count = local + bits
    segments = [jnp.einsum("hqe,hke->hqk", query_units, key_units, precision=highest) * scale]
    gains = [jnp.ones((rows,), jnp.float32)]
    for level in range(1, count):
        unit_scores = (
            jnp.einsum(
                "hqe,hke->hqk", level_queries[level], far_keys_all[level - 1], precision=highest
            )
            * scale
        )
        segments.append(jnp.repeat(unit_scores, 2**level, axis=1))
        gains.append(jnp.full((BLOCK,), 2.0**level, jnp.float32))
    scores = jnp.concatenate(segments, -1)
    peak = jnp.max(scores, -1, keepdims=True)
    weights = jnp.concatenate(gains)[None, None, :] * jnp.exp(scores - peak)
    denom_sum = weights.sum(-1, keepdims=True)
    all_values = jnp.concatenate([value_units] + far_values_all, 1)
    numer_sum = jnp.einsum("hqk,hke->hqe", weights, all_values, precision=highest)
    output = numer_sum / denom_sum
    attn = join_heads(output)
    cotangent = lax.all_gather(out_cotangent, "heads", axis=1, tiled=True)
    d_attn = lax.dot_general(
        cotangent, w_out, (((1,), (1,)), ((), ())), preferred_element_type=jnp.float32
    ).astype(jnp.bfloat16)
    grad_out = split_heads(d_attn)
    delta = jnp.sum(grad_out * output, -1, keepdims=True)
    probs = weights / denom_sum
    inner = jnp.einsum("hqe,hke->hqk", grad_out, all_values, precision=highest)
    dscore = probs * (inner - delta)
    dvalue_all = jnp.einsum("hqk,hqe->hke", probs, grad_out, precision=highest)
    local_dscore = dscore[:, :, :rows]
    query_acc = jnp.einsum("hqk,hke->hqe", local_dscore, key_units, precision=highest) * scale
    key_acc = jnp.einsum("hqk,hqe->hke", local_dscore, query_units, precision=highest) * scale
    value_acc = dvalue_all[:, :rows]
    far_grads = []
    for level in range(1, count):
        factor = 2**level
        start = rows + (level - 1) * BLOCK
        unit_dscore = (
            dscore[:, :, start : start + BLOCK]
            .reshape(heads, rows // factor, factor, BLOCK)
            .sum(2)
        )
        dquery = (
            jnp.einsum(
                "hqk,hke->hqe", unit_dscore, far_keys_all[level - 1], precision=highest
            )
            * scale
        )
        dkey = (
            jnp.einsum("hqk,hqe->hke", unit_dscore, level_queries[level], precision=highest)
            * scale
        )
        far_grads.append((dkey, dvalue_all[:, start : start + BLOCK]))
        query_acc = query_acc + spread_units(dquery, factor)
    carry = None
    for step in reversed(range(bits)):
        send = jnp.concatenate(far_grads[step], 1)
        if carry is not None:
            upper_side = place >> step & 1 == 1
            lower = spread_units(jnp.concatenate([carry[:, :half], carry[:, BLOCK : BLOCK + half]], 1), 2)
            upper = spread_units(jnp.concatenate([carry[:, half:BLOCK], carry[:, BLOCK + half :]], 1), 2)
            send = send + jnp.where(upper_side, lower, upper)
            keep = jnp.where(upper_side, upper, lower)
        else:
            keep = jnp.zeros_like(send)
        carry = keep + partner_2(send, SEQ, step)
    key_acc = key_acc + spread_units(carry[:, :BLOCK], 2**local)
    value_acc = value_acc + spread_units(carry[:, BLOCK:], 2**local)
    norm = 1.0 / math.sqrt(rows * devices)
    outer = lax.psum(1, "sx")
    inner = lax.psum(1, "sz")
    features = cotangent.shape[1]
    block = features // (outer * inner)
    shuffled = cotangent.reshape(rows, outer, inner, block).transpose(0, 2, 1, 3).reshape(rows, features)
    split = attn.shape[1] // 2
    first = (
        lax.dot_general(
            shuffled, attn[:, :split], (((0,), (0,)), ((), ())), preferred_element_type=jnp.float32
        )
        * norm
    )
    second = (
        lax.dot_general(
            cotangent, attn[:, split:], (((0,), (0,)), ((), ())), preferred_element_type=jnp.float32
        )
        * norm
    )
    first = lax.psum_scatter(first, "sz", scatter_dimension=0, tiled=True)
    second = lax.psum_scatter(second, "sx", scatter_dimension=0, tiled=True)
    first = lax.all_to_all(first.reshape(outer, -1, split), "sx", 0, 0).sum(0)
    second = lax.all_to_all(second.reshape(inner, -1, split), "sz", 0, 0).sum(0)
    w_out_grad = jnp.concatenate([first, second], 1)
    return (attn, join_heads(query_acc), join_heads(key_acc), join_heads(value_acc), w_out_grad)


def solution(mesh):
    in_specs = (
        P("seq", "heads"),
        P("seq", "heads"),
        P("seq", "heads"),
        P("heads", None),
        P("seq", "heads"),
    )
    out_specs = (
        P("seq", "heads"),
        P("seq", "heads"),
        P("seq", "heads"),
        P("seq", "heads"),
        P("seq", "heads"),
    )
    zs = sorted({d.coords[2] for d in mesh.devices[:, 0]}) if hasattr(mesh.devices[0, 0], "coords") else [0] * 8
    inner = len(zs) if mesh.shape["seq"] % len(zs) == 0 else 1
    grid = Mesh(mesh.devices.reshape(mesh.shape["seq"] // inner, inner, mesh.shape["heads"]), ("sx", "sz", "heads"))
    in_specs = tuple(P(*[SEQ if a == "seq" else a for a in spec]) for spec in in_specs)
    out_specs = tuple(P(*[SEQ if a == "seq" else a for a in spec]) for spec in out_specs)
    return jax.shard_map(
        per_device, mesh=grid, in_specs=in_specs, out_specs=out_specs, check_vma=False
    )
```

```python
import math

import jax
import jax.numpy as jnp
from jax import lax
from jax.sharding import Mesh, PartitionSpec as P

HEAD_DIM = 128
BLOCK = 128


highest = lax.Precision.HIGHEST


SEQ = ("sx", "sz")


def seq_size():
    return lax.psum(1, SEQ)


def partner_2(x, axis, bit):
    return lax.ppermute(x, axis, [(i, i ^ 1 << bit) for i in range(seq_size())])


def halve_units(field):
    count, units, width = field.shape
    return field.reshape(count, units // 2, 2, width).sum(2) * 0.5


def spread_units(field, factor):
    count, units, width = field.shape
    return jnp.broadcast_to(field[:, :, None, :] / factor, (count, units, factor, width)).reshape(
        count, units * factor, width
    )


def local_terms(query_units, key_units, value_units, level, scale):
    count, units, width = query_units.shape
    pairs = units // (2 * BLOCK)
    query_blocks = query_units.reshape(count, pairs, 2, BLOCK, width)
    key_blocks = key_units.reshape(count, pairs, 2 * BLOCK, width)
    value_blocks = value_units.reshape(count, pairs, 2 * BLOCK, width)
    scores = jnp.einsum("hpsqe,hpke->hpsqk", query_blocks, key_blocks, precision=highest) * scale
    top = jnp.max(scores, -1)
    weights = 2.0**level * jnp.exp(scores - top[..., None])
    numer = jnp.einsum("hpsqk,hpke->hpsqe", weights, value_blocks, precision=highest)
    saved = (query_blocks, key_blocks, value_blocks, weights)
    return (
        top.reshape(count, units),
        numer.reshape(count, units, width),
        weights.sum(-1).reshape(count, units),
        saved,
    )


def local_grads(saved, unit_out, unit_delta, scale):
    query_blocks, key_blocks, value_blocks, weights = saved
    count, pairs, _, block, width = query_blocks.shape
    units = pairs * 2 * block
    grad_blocks = unit_out.reshape(count, pairs, 2, block, width)
    delta_blocks = unit_delta.reshape(count, pairs, 2, block)
    inner = jnp.einsum("hpsqe,hpke->hpsqk", grad_blocks, value_blocks, precision=highest)
    dscore = weights * (inner - delta_blocks[..., None])
    dvalue = jnp.einsum("hpsqk,hpsqe->hpke", weights, grad_blocks, precision=highest)
    dquery = jnp.einsum("hpsqk,hpke->hpsqe", dscore, key_blocks, precision=highest) * scale
    dkey = jnp.einsum("hpsqk,hpsqe->hpke", dscore, query_blocks, precision=highest) * scale
    return (
        dquery.reshape(count, units, width),
        dkey.reshape(count, units, width),
        dvalue.reshape(count, units, width),
    )


def cross_terms(query_units, key_block, value_block, level, scale):
    scores = jnp.einsum("hqe,hke->hqk", query_units, key_block, precision=highest) * scale
    top = jnp.max(scores, -1)
    weights = 2.0**level * jnp.exp(scores - top[..., None])
    numer = jnp.einsum("hqk,hke->hqe", weights, value_block, precision=highest)
    return (top, numer, weights.sum(-1), weights)


def cross_grads(query_units, key_block, value_block, weights, unit_out, unit_delta, scale):
    inner = jnp.einsum("hqe,hke->hqk", unit_out, value_block, precision=highest)
    dscore = weights * (inner - unit_delta[..., None])
    dvalue = jnp.einsum("hqk,hqe->hke", weights, unit_out, precision=highest)
    dquery = jnp.einsum("hqk,hke->hqe", dscore, key_block, precision=highest) * scale
    dkey = jnp.einsum("hqk,hqe->hke", dscore, query_units, precision=highest) * scale
    return (dquery, dkey, dvalue)


def partner(blocks, bit):
    units = blocks[0].shape[1]
    both = partner_2(jnp.concatenate(blocks, 1), SEQ, bit)
    return both[:, :units], both[:, units:]


def partner_grads(blocks, bit):
    return partner(blocks, bit)


def per_device(queries, keys, values, w_out, out_cotangent):
    rows = queries.shape[0]
    heads = queries.shape[1] // HEAD_DIM
    scale = 1.0 / math.sqrt(HEAD_DIM)
    local = (rows // BLOCK).bit_length() - 1
    devices = seq_size()
    bits = devices.bit_length() - 1
    place = lax.axis_index(SEQ)

    def split_heads(field):
        return field.astype(jnp.float32).reshape(rows, heads, HEAD_DIM).transpose(1, 0, 2)

    def join_heads(field):
        return field.transpose(1, 0, 2).reshape(rows, heads * HEAD_DIM).astype(jnp.bfloat16)

    assert local == 1
    query_units = split_heads(queries)
    key_units = split_heads(keys)
    value_units = split_heads(values)
    level_queries = [query_units]
    far_keys_all = []
    far_values_all = []
    query_at = halve_units(query_units)
    own = halve_units(jnp.concatenate([key_units, value_units], 1))
    half = BLOCK // 2
    for step in range(bits):
        if step > 0:
            query_at = halve_units(query_at)
            upper_side = place >> step - 1 & 1 == 1
            lower = halve_units(jnp.where(upper_side, far, own))
            upper = halve_units(jnp.where(upper_side, own, far))
            own = jnp.concatenate(
                [lower[:, :half], upper[:, :half], lower[:, half:], upper[:, half:]], 1
            )
        far = partner_2(own, SEQ, step)
        level_queries.append(query_at)
        far_keys_all.append(far[:, :BLOCK])
        far_values_all.append(far[:, BLOCK:])
    count = local + bits
    segments = [jnp.einsum("hqe,hke->hqk", query_units, key_units, precision=highest) * scale]
    gains = [jnp.ones((rows,), jnp.float32)]
    for level in range(1, count):
        unit_scores = (
            jnp.einsum(
                "hqe,hke->hqk", level_queries[level], far_keys_all[level - 1], precision=highest
            )
            * scale
        )
        segments.append(jnp.repeat(unit_scores, 2**level, axis=1))
        gains.append(jnp.full((BLOCK,), 2.0**level, jnp.float32))
    scores = jnp.concatenate(segments, -1)
    peak = jnp.max(scores, -1, keepdims=True)
    weights = jnp.concatenate(gains)[None, None, :] * jnp.exp(scores - peak)
    denom_sum = weights.sum(-1, keepdims=True)
    all_values = jnp.concatenate([value_units] + far_values_all, 1)
    numer_sum = jnp.einsum("hqk,hke->hqe", weights, all_values, precision=highest)
    output = numer_sum / denom_sum
    attn = join_heads(output)
    cotangent = lax.all_gather(out_cotangent, "heads", axis=1, tiled=True)
    d_attn = lax.dot_general(
        cotangent, w_out, (((1,), (1,)), ((), ())), preferred_element_type=jnp.float32
    ).astype(jnp.bfloat16)
    grad_out = split_heads(d_attn)
    delta = jnp.sum(grad_out * output, -1, keepdims=True)
    probs = weights / denom_sum
    inner = jnp.einsum("hqe,hke->hqk", grad_out, all_values, precision=highest)
    dscore = probs * (inner - delta)
    dvalue_all = jnp.einsum("hqk,hqe->hke", probs, grad_out, precision=highest)
    local_dscore = dscore[:, :, :rows]
    query_acc = jnp.einsum("hqk,hke->hqe", local_dscore, key_units, precision=highest) * scale
    key_acc = jnp.einsum("hqk,hqe->hke", local_dscore, query_units, precision=highest) * scale
    value_acc = dvalue_all[:, :rows]
    far_grads = []
    for level in range(1, count):
        factor = 2**level
        start = rows + (level - 1) * BLOCK
        unit_dscore = (
            dscore[:, :, start : start + BLOCK]
            .reshape(heads, rows // factor, factor, BLOCK)
            .sum(2)
        )
        dquery = (
            jnp.einsum(
                "hqk,hke->hqe", unit_dscore, far_keys_all[level - 1], precision=highest
            )
            * scale
        )
        dkey = (
            jnp.einsum("hqk,hqe->hke", unit_dscore, level_queries[level], precision=highest)
            * scale
        )
        far_grads.append((dkey, dvalue_all[:, start : start + BLOCK]))
        query_acc = query_acc + spread_units(dquery, factor)
    carry = None
    for step in reversed(range(bits)):
        send = jnp.concatenate(far_grads[step], 1)
        if carry is not None:
            upper_side = place >> step & 1 == 1
            lower = spread_units(jnp.concatenate([carry[:, :half], carry[:, BLOCK : BLOCK + half]], 1), 2)
            upper = spread_units(jnp.concatenate([carry[:, half:BLOCK], carry[:, BLOCK + half :]], 1), 2)
            send = send + jnp.where(upper_side, lower, upper)
            keep = jnp.where(upper_side, upper, lower)
        else:
            keep = jnp.zeros_like(send)
        carry = keep + partner_2(send, SEQ, step)
    key_acc = key_acc + spread_units(carry[:, :BLOCK], 2**local)
    value_acc = value_acc + spread_units(carry[:, BLOCK:], 2**local)
    norm = 1.0 / math.sqrt(rows * devices)
    outer = lax.psum(1, "sx")
    inner = lax.psum(1, "sz")
    features = cotangent.shape[1]
    block = features // (outer * inner)
    shuffled = cotangent.reshape(rows, outer, inner, block).transpose(0, 2, 1, 3).reshape(rows, features)
    split = attn.shape[1] * 5 // 8
    first = (
        lax.dot_general(
            shuffled, attn[:, :split], (((0,), (0,)), ((), ())), preferred_element_type=jnp.float32
        )
        * norm
    )
    second = (
        lax.dot_general(
            cotangent, attn[:, split:], (((0,), (0,)), ((), ())), preferred_element_type=jnp.float32
        )
        * norm
    )
    first = lax.psum_scatter(first, "sz", scatter_dimension=0, tiled=True)
    second = lax.psum_scatter(second, "sx", scatter_dimension=0, tiled=True)
    first = lax.all_to_all(first.reshape(outer, -1, first.shape[1]), "sx", 0, 0).sum(0)
    second = lax.all_to_all(second.reshape(inner, -1, second.shape[1]), "sz", 0, 0).sum(0)
    w_out_grad = jnp.concatenate([first, second], 1)
    return (attn, join_heads(query_acc), join_heads(key_acc), join_heads(value_acc), w_out_grad)


def solution(mesh):
    in_specs = (
        P("seq", "heads"),
        P("seq", "heads"),
        P("seq", "heads"),
        P("heads", None),
        P("seq", "heads"),
    )
    out_specs = (
        P("seq", "heads"),
        P("seq", "heads"),
        P("seq", "heads"),
        P("seq", "heads"),
        P("seq", "heads"),
    )
    zs = sorted({d.coords[2] for d in mesh.devices[:, 0]}) if hasattr(mesh.devices[0, 0], "coords") else [0] * 8
    inner = len(zs) if mesh.shape["seq"] % len(zs) == 0 else 1
    grid = Mesh(mesh.devices.reshape(mesh.shape["seq"] // inner, inner, mesh.shape["heads"]), ("sx", "sz", "heads"))
    in_specs = tuple(P(*[SEQ if a == "seq" else a for a in spec]) for spec in in_specs)
    out_specs = tuple(P(*[SEQ if a == "seq" else a for a in spec]) for spec in out_specs)
    return jax.shard_map(
        per_device, mesh=grid, in_specs=in_specs, out_specs=out_specs, check_vma=False
    )
```

```python
import math

import jax
import jax.numpy as jnp
from jax import lax
from jax.sharding import Mesh, PartitionSpec as P

HEAD_DIM = 128
BLOCK = 128


highest = lax.Precision.HIGHEST


SEQ = ("sx", "sz")


def seq_size():
    return lax.psum(1, SEQ)


def partner_2(x, axis, bit):
    return lax.ppermute(x, axis, [(i, i ^ 1 << bit) for i in range(seq_size())])


def halve_units(field):
    count, units, width = field.shape
    return field.reshape(count, units // 2, 2, width).sum(2) * 0.5


def spread_units(field, factor):
    count, units, width = field.shape
    return jnp.broadcast_to(field[:, :, None, :] / factor, (count, units, factor, width)).reshape(
        count, units * factor, width
    )


def local_terms(query_units, key_units, value_units, level, scale):
    count, units, width = query_units.shape
    pairs = units // (2 * BLOCK)
    query_blocks = query_units.reshape(count, pairs, 2, BLOCK, width)
    key_blocks = key_units.reshape(count, pairs, 2 * BLOCK, width)
    value_blocks = value_units.reshape(count, pairs, 2 * BLOCK, width)
    scores = jnp.einsum("hpsqe,hpke->hpsqk", query_blocks, key_blocks, precision=highest) * scale
    top = jnp.max(scores, -1)
    weights = 2.0**level * jnp.exp(scores - top[..., None])
    numer = jnp.einsum("hpsqk,hpke->hpsqe", weights, value_blocks, precision=highest)
    saved = (query_blocks, key_blocks, value_blocks, weights)
    return (
        top.reshape(count, units),
        numer.reshape(count, units, width),
        weights.sum(-1).reshape(count, units),
        saved,
    )


def local_grads(saved, unit_out, unit_delta, scale):
    query_blocks, key_blocks, value_blocks, weights = saved
    count, pairs, _, block, width = query_blocks.shape
    units = pairs * 2 * block
    grad_blocks = unit_out.reshape(count, pairs, 2, block, width)
    delta_blocks = unit_delta.reshape(count, pairs, 2, block)
    inner = jnp.einsum("hpsqe,hpke->hpsqk", grad_blocks, value_blocks, precision=highest)
    dscore = weights * (inner - delta_blocks[..., None])
    dvalue = jnp.einsum("hpsqk,hpsqe->hpke", weights, grad_blocks, precision=highest)
    dquery = jnp.einsum("hpsqk,hpke->hpsqe", dscore, key_blocks, precision=highest) * scale
    dkey = jnp.einsum("hpsqk,hpsqe->hpke", dscore, query_blocks, precision=highest) * scale
    return (
        dquery.reshape(count, units, width),
        dkey.reshape(count, units, width),
        dvalue.reshape(count, units, width),
    )


def cross_terms(query_units, key_block, value_block, level, scale):
    scores = jnp.einsum("hqe,hke->hqk", query_units, key_block, precision=highest) * scale
    top = jnp.max(scores, -1)
    weights = 2.0**level * jnp.exp(scores - top[..., None])
    numer = jnp.einsum("hqk,hke->hqe", weights, value_block, precision=highest)
    return (top, numer, weights.sum(-1), weights)


def cross_grads(query_units, key_block, value_block, weights, unit_out, unit_delta, scale):
    inner = jnp.einsum("hqe,hke->hqk", unit_out, value_block, precision=highest)
    dscore = weights * (inner - unit_delta[..., None])
    dvalue = jnp.einsum("hqk,hqe->hke", weights, unit_out, precision=highest)
    dquery = jnp.einsum("hqk,hke->hqe", dscore, key_block, precision=highest) * scale
    dkey = jnp.einsum("hqk,hqe->hke", dscore, query_units, precision=highest) * scale
    return (dquery, dkey, dvalue)


def partner(blocks, bit):
    units = blocks[0].shape[1]
    both = partner_2(jnp.concatenate(blocks, 1), SEQ, bit)
    return both[:, :units], both[:, units:]


def partner_grads(blocks, bit):
    return partner(blocks, bit)


def per_device(queries, keys, values, w_out, out_cotangent):
    rows = queries.shape[0]
    heads = queries.shape[1] // HEAD_DIM
    scale = 1.0 / math.sqrt(HEAD_DIM)
    local = (rows // BLOCK).bit_length() - 1
    devices = seq_size()
    bits = devices.bit_length() - 1
    place = lax.axis_index(SEQ)

    def split_heads(field):
        return field.astype(jnp.float32).reshape(rows, heads, HEAD_DIM).transpose(1, 0, 2)

    def join_heads(field):
        return field.transpose(1, 0, 2).reshape(rows, heads * HEAD_DIM).astype(jnp.bfloat16)

    assert local == 1
    query_units = split_heads(queries)
    key_units = split_heads(keys)
    value_units = split_heads(values)
    level_queries = [query_units]
    far_keys_all = []
    far_values_all = []
    query_at = halve_units(query_units)
    own = halve_units(jnp.concatenate([key_units, value_units], 1))
    half = BLOCK // 2
    for step in range(bits):
        if step > 0:
            query_at = halve_units(query_at)
            upper_side = place >> step - 1 & 1 == 1
            lower = halve_units(jnp.where(upper_side, far, own))
            upper = halve_units(jnp.where(upper_side, own, far))
            own = jnp.concatenate(
                [lower[:, :half], upper[:, :half], lower[:, half:], upper[:, half:]], 1
            )
        far = partner_2(own, SEQ, step)
        level_queries.append(query_at)
        far_keys_all.append(far[:, :BLOCK])
        far_values_all.append(far[:, BLOCK:])
    count = local + bits
    segments = [jnp.einsum("hqe,hke->hqk", query_units, key_units, precision=highest) * scale]
    gains = [jnp.ones((rows,), jnp.float32)]
    for level in range(1, count):
        unit_scores = (
            jnp.einsum(
                "hqe,hke->hqk", level_queries[level], far_keys_all[level - 1], precision=highest
            )
            * scale
        )
        segments.append(jnp.repeat(unit_scores, 2**level, axis=1))
        gains.append(jnp.full((BLOCK,), 2.0**level, jnp.float32))
    scores = jnp.concatenate(segments, -1)
    peak = jnp.max(scores, -1, keepdims=True)
    weights = jnp.concatenate(gains)[None, None, :] * jnp.exp(scores - peak)
    denom_sum = weights.sum(-1, keepdims=True)
    all_values = jnp.concatenate([value_units] + far_values_all, 1)
    numer_sum = jnp.einsum("hqk,hke->hqe", weights, all_values, precision=highest)
    output = numer_sum / denom_sum
    attn = join_heads(output)
    cotangent = lax.all_gather(out_cotangent, "heads", axis=1, tiled=True)
    d_attn = lax.dot_general(
        cotangent, w_out, (((1,), (1,)), ((), ())), preferred_element_type=jnp.float32
    ).astype(jnp.bfloat16)
    grad_out = split_heads(d_attn)
    delta = jnp.sum(grad_out * output, -1, keepdims=True)
    probs = weights / denom_sum
    inner = jnp.einsum("hqe,hke->hqk", grad_out, all_values, precision=highest)
    dscore = probs * (inner - delta)
    dvalue_all = jnp.einsum("hqk,hqe->hke", probs, grad_out, precision=highest)
    local_dscore = dscore[:, :, :rows]
    query_acc = jnp.einsum("hqk,hke->hqe", local_dscore, key_units, precision=highest) * scale
    key_acc = jnp.einsum("hqk,hqe->hke", local_dscore, query_units, precision=highest) * scale
    value_acc = dvalue_all[:, :rows]
    far_grads = []
    for level in range(1, count):
        factor = 2**level
        start = rows + (level - 1) * BLOCK
        unit_dscore = (
            dscore[:, :, start : start + BLOCK]
            .reshape(heads, rows // factor, factor, BLOCK)
            .sum(2)
        )
        dquery = (
            jnp.einsum(
                "hqk,hke->hqe", unit_dscore, far_keys_all[level - 1], precision=highest
            )
            * scale
        )
        dkey = (
            jnp.einsum("hqk,hqe->hke", unit_dscore, level_queries[level], precision=highest)
            * scale
        )
        far_grads.append((dkey, dvalue_all[:, start : start + BLOCK]))
        query_acc = query_acc + spread_units(dquery, factor)
    carry = None
    for step in reversed(range(bits)):
        send = jnp.concatenate(far_grads[step], 1)
        if carry is not None:
            upper_side = place >> step & 1 == 1
            lower = spread_units(jnp.concatenate([carry[:, :half], carry[:, BLOCK : BLOCK + half]], 1), 2)
            upper = spread_units(jnp.concatenate([carry[:, half:BLOCK], carry[:, BLOCK + half :]], 1), 2)
            send = send + jnp.where(upper_side, lower, upper)
            keep = jnp.where(upper_side, upper, lower)
        else:
            keep = jnp.zeros_like(send)
        carry = keep + partner_2(send, SEQ, step)
    key_acc = key_acc + spread_units(carry[:, :BLOCK], 2**local)
    value_acc = value_acc + spread_units(carry[:, BLOCK:], 2**local)
    norm = 1.0 / math.sqrt(rows * devices)
    outer = lax.psum(1, "sx")
    inner = lax.psum(1, "sz")
    features = cotangent.shape[1]
    block = features // (outer * inner)
    shuffled = cotangent.reshape(rows, outer, inner, block).transpose(0, 2, 1, 3).reshape(rows, features)
    split = attn.shape[1] * 3 // 8
    first = (
        lax.dot_general(
            shuffled, attn[:, :split], (((0,), (0,)), ((), ())), preferred_element_type=jnp.float32
        )
        * norm
    )
    second = (
        lax.dot_general(
            cotangent, attn[:, split:], (((0,), (0,)), ((), ())), preferred_element_type=jnp.float32
        )
        * norm
    )
    first = lax.psum_scatter(first, "sz", scatter_dimension=0, tiled=True)
    second = lax.psum_scatter(second, "sx", scatter_dimension=0, tiled=True)
    first = lax.all_to_all(first.reshape(outer, -1, first.shape[1]), "sx", 0, 0).sum(0)
    second = lax.all_to_all(second.reshape(inner, -1, second.shape[1]), "sz", 0, 0).sum(0)
    w_out_grad = jnp.concatenate([first, second], 1)
    return (attn, join_heads(query_acc), join_heads(key_acc), join_heads(value_acc), w_out_grad)


def solution(mesh):
    in_specs = (
        P("seq", "heads"),
        P("seq", "heads"),
        P("seq", "heads"),
        P("heads", None),
        P("seq", "heads"),
    )
    out_specs = (
        P("seq", "heads"),
        P("seq", "heads"),
        P("seq", "heads"),
        P("seq", "heads"),
        P("seq", "heads"),
    )
    zs = sorted({d.coords[2] for d in mesh.devices[:, 0]}) if hasattr(mesh.devices[0, 0], "coords") else [0] * 8
    inner = len(zs) if mesh.shape["seq"] % len(zs) == 0 else 1
    grid = Mesh(mesh.devices.reshape(mesh.shape["seq"] // inner, inner, mesh.shape["heads"]), ("sx", "sz", "heads"))
    in_specs = tuple(P(*[SEQ if a == "seq" else a for a in spec]) for spec in in_specs)
    out_specs = tuple(P(*[SEQ if a == "seq" else a for a in spec]) for spec in out_specs)
    return jax.shard_map(
        per_device, mesh=grid, in_specs=in_specs, out_specs=out_specs, check_vma=False
    )
```
